256 devices in a mesh: sample: 8 (over z_lo, x), lat: 32 (over z_hi, y, core).
Axes of the slice: x: 4, y: 4, z: 8 (z_hi: 4, z_lo: 2; z = z_hi * 2 + z_lo), core: 2. Of those that a mesh axis runs over, the one named last changes fastest.
Arguments:
- tokens: bfloat16 [8, 96, 180, 768], P('sample', 'lat'), may hold values from -6 to 6
- norm_gain: float32 [768], replicated, may hold values from 0.5 to 1.5
- norm_shift: float32 [768], replicated, may hold values from -0.5 to 0.5
- weight_one: float32 [2, 8, 96, 96], replicated, may hold values from -0.4375 to 0.4375
- bias_one: float32 [2, 8, 96], replicated, may hold values from -3 to 3
- weight_two: float32 [2, 8, 96, 96], replicated, may hold values from -0.4375 to 0.4375
- bias_two: float32 [2, 8, 96], replicated, may hold values from -0.12 to 0.12
- cotangent: bfloat16 [8, 96, 180, 768], P('sample', 'lat'), may hold values from -6 to 6
Outputs:
- block_out: bfloat16 [8, 96, 180, 768], P('sample', 'lat')
- grad_input: bfloat16 [8, 96, 180, 768], P('sample', 'lat')
- grad_gain: float32 [768], replicated
- grad_shift: float32 [768], replicated
- grad_weight_one: float32 [2, 8, 96, 96], replicated
- grad_bias_one: float32 [2, 8, 96], replicated
- grad_weight_two: float32 [2, 8, 96, 96], replicated
- grad_bias_two: float32 [2, 8, 96], replicated
The draws below stay inside these ranges and needn't reach their ends.
All inputs are finite; a program needn't handle non-finite values.
Results may differ from the reference program's by a relative error of at most 0.001.
Values sent between devices are 32-bit elements; how exact they have to be, the bound alone decides.
No kernel may reach another device: no remote copies, remote signals or barrier semaphores. Data moves between devices by JAX's collectives and lax.ppermute only.
A program may use at most 128 MiB of HBM per device.

```python
import jax
import jax.numpy as jnp
from jax import lax

C = 768
G = 8
H = 96
W = 180
BLOCK = 96
B = 8


def shard_levels(key, shape, shards, low, largest):
    loudness, own = 1.0, jax.random.fold_in(key, 6)
    for dim, blocks in shards:
        steps = jnp.exp(jax.random.uniform(jax.random.fold_in(own, dim), (blocks,), jnp.float32, low / len(shards), largest / len(shards)))
        loudness = loudness * jnp.repeat(steps, shape[dim] // blocks).reshape([-1 if axis == dim else 1 for axis in range(len(shape))])
    return loudness


def noise(rng, shape, deviation, bound, cuts=(), kind=jnp.bfloat16):
    drawn = jax.random.normal(rng, shape, jnp.float32) * deviation
    if len(cuts) > 0:
        drawn = shard_levels(rng, shape, cuts, -0.22, 0.18) * drawn
    return jnp.clip(drawn, min=-bound, max=bound).astype(kind)


def setup_inputs(seed: int = 0) -> dict:
    seeds = jax.random.split(jax.random.key(seed), 9)
    tokens = noise(seeds[0], (B, H, W, C), 1.0, 6.0, ((0, 8), (1, 32)))
    norm_gain = jnp.clip(1.0 + 0.1 * jax.random.normal(seeds[1], (C,), jnp.float32), 0.5, 1.5)
    norm_shift = jnp.clip(jax.random.uniform(seeds[2], (C,), jnp.float32, -0.5, 0.5), -0.5, 0.5)
    weight_one = noise(seeds[3], (2, G, BLOCK, BLOCK), (2 * BLOCK) ** -0.5, 0.4375, (), jnp.float32)
    bias_one = noise(seeds[4], (2, G, BLOCK), 0.5, 3.0, (), jnp.float32)
    weight_two = noise(seeds[5], (2, G, BLOCK, BLOCK), (2 * BLOCK) ** -0.5, 0.4375, (), jnp.float32)
    bias_two = noise(seeds[6], (2, G, BLOCK), 0.02, 0.12, (), jnp.float32)
    cotangent = noise(seeds[7], (B, H, W, C), 1.0, 6.0, ((0, 8), (1, 32)))
    return {"tokens": tokens, "norm_gain": norm_gain, "norm_shift": norm_shift, "weight_one": weight_one, "bias_one": bias_one, "weight_two": weight_two, "bias_two": bias_two, "cotangent": cotangent}


HIGHEST = lax.Precision.HIGHEST
SHRINK = 0.01
EPSILON = 1e-05

def lon_basis(cell_count, mode_count):
    cell_index = jnp.arange(cell_count, dtype=jnp.int32)[:, None]
    mode_index = jnp.arange(mode_count, dtype=jnp.int32)[None, :]
    phase_int = (cell_index * mode_index % cell_count).astype(jnp.float32)
    phase_angle = phase_int * (2.0 * jnp.pi / cell_count)
    keep_scale = (mode_index < cell_count // 2 + 1).astype(jnp.float32) / jnp.sqrt(jnp.float32(cell_count))
    return jnp.stack([jnp.cos(phase_angle) * keep_scale, -jnp.sin(phase_angle) * keep_scale], axis=1)

def lon_weight(cell_count, mode_count):
    mode_index = jnp.arange(mode_count, dtype=jnp.int32)
    single = jnp.logical_or(mode_index == 0, 2 * mode_index == cell_count)
    return jnp.where(single, 1.0, 2.0).astype(jnp.float32)

def lat_basis(row_count):
    row_index = jnp.arange(row_count, dtype=jnp.int32)
    phase_int = (row_index[:, None] * row_index[None, :] % row_count).astype(jnp.float32)
    phase_angle = phase_int * (2.0 * jnp.pi / row_count)
    norm_factor = 1.0 / jnp.sqrt(jnp.float32(row_count))
    return (jnp.cos(phase_angle) * norm_factor, jnp.sin(phase_angle) * norm_factor)

def lat_apply(values_in, cosine, sine_table, orient):
    cosine_part = jnp.einsum('ph,hrkc->prkc', cosine, values_in, precision=HIGHEST)
    sine_part = jnp.einsum('ph,hrkc->prkc', sine_table, values_in, precision=HIGHEST)
    real_part = cosine_part[:, 0] + orient * sine_part[:, 1]
    imag_part = cosine_part[:, 1] - orient * sine_part[:, 0]
    return jnp.stack([real_part, imag_part], axis=1)

def block_product(values_in, weights):

    def product_part(part_in, slot_index):
        return jnp.einsum('hkgi,gio->hkgo', part_in, weights[slot_index], precision=HIGHEST)
    real_input = values_in[:, 0]
    imag_input = values_in[:, 1]
    real_out = product_part(real_input, 0) - product_part(imag_input, 1)
    imag_out = product_part(imag_input, 0) + product_part(real_input, 1)
    return jnp.stack([real_out, imag_out], axis=1)

def shrink(values):
    return values - SHRINK * values * lax.rsqrt(values * values + SHRINK * SHRINK)

def block_forward(float_tokens, norm_gain, norm_shift, weight_one, bias_one, weight_two, bias_two):
    row_count, cell_count, feature_count = float_tokens.shape
    group_count = weight_one.shape[1]
    block_size = weight_one.shape[2]
    kept_modes = cell_count // 2 + 1
    lon_table = lon_basis(cell_count, kept_modes)
    weighted = lon_table * lon_weight(cell_count, kept_modes)[None, None, :]
    cosine, sine_table = lat_basis(row_count)
    average = lax.optimization_barrier(jnp.mean(float_tokens, axis=-1, keepdims=True))
    centred = float_tokens - average
    variance = lax.optimization_barrier(jnp.mean(centred * centred, axis=-1, keepdims=True))
    normed = centred * lax.rsqrt(variance + EPSILON) * norm_gain + norm_shift
    lon_spectrum = jnp.einsum('hwc,wrk->hrkc', normed, lon_table, precision=HIGHEST)
    spectrum = lat_apply(lon_spectrum, cosine, sine_table, 1.0)
    grouped = spectrum.reshape((row_count, 2, kept_modes, group_count, block_size))
    inner_act = jax.nn.gelu(block_product(grouped, weight_one) + bias_one[None, :, None])
    outer_act = block_product(inner_act, weight_two) + bias_two[None, :, None]
    shrunk = shrink(outer_act).reshape((row_count, 2, kept_modes, feature_count))
    lat_back = lat_apply(shrunk, cosine, sine_table, -1.0)
    filtered = jnp.einsum('hrkc,wrk->hwc', lat_back, weighted, precision=HIGHEST)
    return float_tokens + normed + filtered

def reference(tokens, norm_gain, norm_shift, weight_one, bias_one, weight_two, bias_two, cotangent):

    def one_sample(sample_pair):
        sample_tokens, sample_cotangent = sample_pair
        result, pullback = jax.vjp(block_forward, sample_tokens.astype(jnp.float32), norm_gain, norm_shift, weight_one, bias_one, weight_two, bias_two)
        gradients = pullback(sample_cotangent.astype(jnp.float32))
        return (result.astype(jnp.bfloat16), gradients[0].astype(jnp.bfloat16), gradients[1:])
    block_out, grad_input, remaining = lax.map(one_sample, (tokens, cotangent))
    summed = [lax.optimization_barrier(jnp.sum(member, axis=0)) for member in remaining]
    return (block_out, grad_input, summed[0], summed[1], summed[2], summed[3], summed[4], summed[5])
```

```python
import jax
import jax.numpy as jnp
from jax import lax
from jax.sharding import PartitionSpec as P

HIGHEST = lax.Precision.HIGHEST
SHRINK = 0.01
EPSILON = 1e-05


def lon_basis(cell_count, mode_count):
    cell_index = jnp.arange(cell_count, dtype=jnp.int32)[:, None]
    mode_index = jnp.arange(mode_count, dtype=jnp.int32)[None, :]
    phase_int = (cell_index * mode_index % cell_count).astype(jnp.float32)
    phase_angle = phase_int * (2.0 * jnp.pi / cell_count)
    keep_scale = (mode_index < cell_count // 2 + 1).astype(jnp.float32) / jnp.sqrt(
        jnp.float32(cell_count)
    )
    return jnp.stack(
        [jnp.cos(phase_angle) * keep_scale, -jnp.sin(phase_angle) * keep_scale], axis=1
    )


def lon_weight(cell_count, mode_count):
    mode_index = jnp.arange(mode_count, dtype=jnp.int32)
    single = jnp.logical_or(mode_index == 0, 2 * mode_index == cell_count)
    return jnp.where(single, 1.0, 2.0).astype(jnp.float32)


def lat_basis(row_count):
    row_index = jnp.arange(row_count, dtype=jnp.int32)
    phase_int = (row_index[:, None] * row_index[None, :] % row_count).astype(jnp.float32)
    phase_angle = phase_int * (2.0 * jnp.pi / row_count)
    norm_factor = 1.0 / jnp.sqrt(jnp.float32(row_count))
    return (jnp.cos(phase_angle) * norm_factor, jnp.sin(phase_angle) * norm_factor)


def lat_apply(values_in, cosine, sine_table, orient):
    cosine_part = jnp.einsum("ph,shrkc->sprkc", cosine, values_in, precision=HIGHEST)
    sine_part = jnp.einsum("ph,shrkc->sprkc", sine_table, values_in, precision=HIGHEST)
    real_part = cosine_part[:, :, 0] + orient * sine_part[:, :, 1]
    imag_part = cosine_part[:, :, 1] - orient * sine_part[:, :, 0]
    return jnp.stack([real_part, imag_part], axis=2)


def block_product(values_in, weights):

    def product_part(part_in, slot_index):
        return jnp.einsum("shkgi,gio->shkgo", part_in, weights[slot_index], precision=HIGHEST)

    real_input = values_in[:, :, 0]
    imag_input = values_in[:, :, 1]
    real_out = product_part(real_input, 0) - product_part(imag_input, 1)
    imag_out = product_part(imag_input, 0) + product_part(real_input, 1)
    return jnp.stack([real_out, imag_out], axis=2)


def block_adjoint(values_in, weights):

    def product_part(part_in, slot_index):
        return jnp.einsum("shkgo,gio->shkgi", part_in, weights[slot_index], precision=HIGHEST)

    real_input = values_in[:, :, 0]
    imag_input = values_in[:, :, 1]
    real_out = product_part(real_input, 0) + product_part(imag_input, 1)
    imag_out = product_part(imag_input, 0) - product_part(real_input, 1)
    return jnp.stack([real_out, imag_out], axis=2)


def weight_grad(inputs, upstream):

    def contract(left_side, right_side):
        return jnp.einsum("shkgi,shkgo->gio", left_side, right_side, precision=HIGHEST)

    real_input = inputs[:, :, 0]
    imag_input = inputs[:, :, 1]
    real_upper = upstream[:, :, 0]
    imag_upper = upstream[:, :, 1]
    first = contract(real_input, real_upper) + contract(imag_input, imag_upper)
    second = contract(real_input, imag_upper) - contract(imag_input, real_upper)
    return jnp.stack([first, second], axis=0)


def shrink(values):
    return values - SHRINK * values * lax.rsqrt(values * values + SHRINK * SHRINK)


def flat_sum(parts, axes):
    count = 1
    for name in axes:
        count *= lax.axis_size(name)
    flat = jnp.concatenate([part.reshape(-1) for part in parts])
    size = flat.shape[0]
    chunk = -(-size // (count * 128)) * 128
    flat = jnp.pad(flat, (0, count * chunk - size)).reshape(count, chunk)
    reduced = lax.all_to_all(flat, axes, 0, 0, tiled=True).sum(axis=0)
    spread = jnp.broadcast_to(reduced[None], (count, chunk))
    whole = lax.all_to_all(spread, axes, 0, 0, tiled=True).reshape(-1)
    results = []
    offset = 0
    for part in parts:
        results.append(whole[offset : offset + part.size].reshape(part.shape))
        offset += part.size
    return tuple(results)


def local(tokens, norm_gain, norm_shift, weight_one, bias_one, weight_two, bias_two, cotangent):
    lat_parts = lax.axis_size("lat")
    samples, local_rows, lon_cells, features = tokens.shape
    groups = weight_one.shape[1]
    block_size = weight_one.shape[2]
    lat_rows = local_rows * lat_parts
    kept_modes = lon_cells // 2 + 1
    padded = (kept_modes + lat_parts - 1) // lat_parts * lat_parts
    lon_table = lon_basis(lon_cells, padded)
    weighted = lon_table * lon_weight(lon_cells, padded)[None, None, :]
    cosine, sine_table = lat_basis(lat_rows)
    float_tokens = tokens.astype(jnp.float32)
    average = jnp.mean(float_tokens, axis=-1, keepdims=True)
    centred = float_tokens - average
    variance = jnp.mean(centred * centred, axis=-1, keepdims=True)
    inverse_std = lax.rsqrt(variance + EPSILON)
    normalized = centred * inverse_std
    normed = normalized * norm_gain + norm_shift
    upstream_out = cotangent.astype(jnp.float32)
    lon_spectrum = jnp.einsum("shwc,wrk->shrkc", normed, lon_table, precision=HIGHEST)
    cotangent_lon = jnp.einsum("shwc,wrk->shrkc", upstream_out, weighted, precision=HIGHEST)
    mode_shape = (samples, lat_rows, 2, padded // lat_parts, groups, block_size)
    gathered = lax.all_to_all(lon_spectrum, "lat", split_axis=3, concat_axis=1, tiled=True)
    spectrum = lat_apply(gathered, cosine, sine_table, 1.0).reshape(mode_shape)
    pre_inner = block_product(spectrum, weight_one) + bias_one[None, None, :, None]
    inner_act, gelu_back = jax.vjp(jax.nn.gelu, pre_inner)
    pre_outer = block_product(inner_act, weight_two) + bias_two[None, None, :, None]
    shrunk, shrink_back = jax.vjp(shrink, pre_outer)
    leaving = lat_apply(shrunk.reshape(gathered.shape), cosine, sine_table, -1.0)
    leaving, saved_state = (leaving, (spectrum, inner_act, gelu_back, shrink_back))
    returned = lax.all_to_all(leaving, "lat", split_axis=1, concat_axis=3, tiled=True)
    cotangent_modes = lax.all_to_all(cotangent_lon, "lat", split_axis=3, concat_axis=1, tiled=True)
    spectrum, inner_act, gelu_back, shrink_back = saved_state
    shrunk_grad = lat_apply(cotangent_modes, cosine, sine_table, 1.0).reshape(mode_shape)
    outer_grad = shrink_back(shrunk_grad)[0]
    weight_two_grad = weight_grad(inner_act, outer_grad)
    bias_two_grad = jnp.sum(outer_grad, axis=(0, 1, 3))
    inner_grad = gelu_back(block_adjoint(outer_grad, weight_two))[0]
    weight_one_grad = weight_grad(spectrum, inner_grad)
    bias_one_grad = jnp.sum(inner_grad, axis=(0, 1, 3))
    spectrum_grad = block_adjoint(inner_grad, weight_one).reshape(cotangent_modes.shape)
    adjoint_modes = lat_apply(spectrum_grad, cosine, sine_table, -1.0)
    adjoint_modes, spectral_grads = (
        adjoint_modes,
        (weight_one_grad, bias_one_grad, weight_two_grad, bias_two_grad),
    )
    adjoint_rows = lax.all_to_all(adjoint_modes, "lat", split_axis=1, concat_axis=3, tiled=True)
    filtered = jnp.einsum("shrkc,wrk->shwc", returned, weighted, precision=HIGHEST)
    block_out = (float_tokens + normed + filtered).astype(jnp.bfloat16)
    normed_grad = upstream_out + jnp.einsum(
        "shrkc,wrk->shwc", adjoint_rows, lon_table, precision=HIGHEST
    )
    hat_grad = normed_grad * norm_gain
    hat_mean = jnp.mean(hat_grad, axis=-1, keepdims=True)
    cross_mean = jnp.mean(hat_grad * normalized, axis=-1, keepdims=True)
    grad_input = upstream_out + inverse_std * (hat_grad - hat_mean - normalized * cross_mean)
    local_gain = jnp.sum(normed_grad * normalized, axis=(0, 1, 2))
    local_shift = jnp.sum(normed_grad, axis=(0, 1, 2))
    summed = flat_sum(
        (
            spectral_grads[0],
            spectral_grads[1],
            spectral_grads[2],
            spectral_grads[3],
            local_gain,
            local_shift,
        ),
        ("sample", "lat"),
    )
    return (
        block_out,
        grad_input.astype(jnp.bfloat16),
        summed[4],
        summed[5],
        summed[0],
        summed[1],
        summed[2],
        summed[3],
    )


def solution(mesh):
    placed = (
        P("sample", "lat", None, None),
        P(),
        P(),
        P(),
        P(),
        P(),
        P(),
        P("sample", "lat", None, None),
    )
    return jax.shard_map(
        local,
        mesh=mesh,
        in_specs=placed,
        out_specs=(
            P("sample", "lat", None, None),
            P("sample", "lat", None, None),
            P(),
            P(),
            P(),
            P(),
            P(),
            P(),
        ),
        check_vma=False,
    )
```

```python
import jax
import jax.numpy as jnp
from jax import lax
from jax.sharding import PartitionSpec as P

HIGHEST = lax.Precision.HIGHEST
SHRINK = 0.01
EPSILON = 1e-05


def lon_basis(cell_count, mode_count):
    cell_index = jnp.arange(cell_count, dtype=jnp.int32)[:, None]
    mode_index = jnp.arange(mode_count, dtype=jnp.int32)[None, :]
    phase_int = (cell_index * mode_index % cell_count).astype(jnp.float32)
    phase_angle = phase_int * (2.0 * jnp.pi / cell_count)
    keep_scale = (mode_index < cell_count // 2 + 1).astype(jnp.float32) / jnp.sqrt(
        jnp.float32(cell_count)
    )
    return jnp.stack(
        [jnp.cos(phase_angle) * keep_scale, -jnp.sin(phase_angle) * keep_scale], axis=1
    )


def lon_weight(cell_count, mode_count):
    mode_index = jnp.arange(mode_count, dtype=jnp.int32)
    single = jnp.logical_or(mode_index == 0, 2 * mode_index == cell_count)
    return jnp.where(single, 1.0, 2.0).astype(jnp.float32)


def lat_basis(row_count):
    row_index = jnp.arange(row_count, dtype=jnp.int32)
    phase_int = (row_index[:, None] * row_index[None, :] % row_count).astype(jnp.float32)
    phase_angle = phase_int * (2.0 * jnp.pi / row_count)
    norm_factor = 1.0 / jnp.sqrt(jnp.float32(row_count))
    return (jnp.cos(phase_angle) * norm_factor, jnp.sin(phase_angle) * norm_factor)


def lat_apply(values_in, cosine, sine_table, orient):
    cosine_part = jnp.einsum("ph,shrkc->sprkc", cosine, values_in, precision=HIGHEST)
    sine_part = jnp.einsum("ph,shrkc->sprkc", sine_table, values_in, precision=HIGHEST)
    real_part = cosine_part[:, :, 0] + orient * sine_part[:, :, 1]
    imag_part = cosine_part[:, :, 1] - orient * sine_part[:, :, 0]
    return jnp.stack([real_part, imag_part], axis=2)


def block_product(values_in, weights):

    def product_part(part_in, slot_index):
        return jnp.einsum("shkgi,gio->shkgo", part_in, weights[slot_index], precision=HIGHEST)

    real_input = values_in[:, :, 0]
    imag_input = values_in[:, :, 1]
    real_out = product_part(real_input, 0) - product_part(imag_input, 1)
    imag_out = product_part(imag_input, 0) + product_part(real_input, 1)
    return jnp.stack([real_out, imag_out], axis=2)


def block_adjoint(values_in, weights):

    def product_part(part_in, slot_index):
        return jnp.einsum("shkgo,gio->shkgi", part_in, weights[slot_index], precision=HIGHEST)

    real_input = values_in[:, :, 0]
    imag_input = values_in[:, :, 1]
    real_out = product_part(real_input, 0) + product_part(imag_input, 1)
    imag_out = product_part(imag_input, 0) - product_part(real_input, 1)
    return jnp.stack([real_out, imag_out], axis=2)


def weight_grad(inputs, upstream):

    def contract(left_side, right_side):
        return jnp.einsum("shkgi,shkgo->gio", left_side, right_side, precision=HIGHEST)

    real_input = inputs[:, :, 0]
    imag_input = inputs[:, :, 1]
    real_upper = upstream[:, :, 0]
    imag_upper = upstream[:, :, 1]
    first = contract(real_input, real_upper) + contract(imag_input, imag_upper)
    second = contract(real_input, imag_upper) - contract(imag_input, real_upper)
    return jnp.stack([first, second], axis=0)


def shrink(values):
    return values - SHRINK * values * lax.rsqrt(values * values + SHRINK * SHRINK)


def flat_sum(parts, axes):
    count = 1
    for name in axes:
        count *= lax.axis_size(name)
    flat = jnp.concatenate([part.reshape(-1) for part in parts])
    size = flat.shape[0]
    chunk = -(-size // (count * 128)) * 128
    flat = jnp.pad(flat, (0, count * chunk - size)).reshape(count, chunk)
    reduced = lax.all_to_all(flat, axes, 0, 0, tiled=True).sum(axis=0)
    spread = jnp.broadcast_to(reduced[None], (count, chunk))
    whole = lax.all_to_all(spread, axes, 0, 0, tiled=True).reshape(-1)
    results = []
    offset = 0
    for part in parts:
        results.append(whole[offset : offset + part.size].reshape(part.shape))
        offset += part.size
    return tuple(results)


def lat_in(values_in, cosine_in, sine_in, orient):
    cosine_part = jnp.einsum("pjh,jshrmc->sprmc", cosine_in, values_in, precision=HIGHEST)
    sine_part = jnp.einsum("pjh,jshrmc->sprmc", sine_in, values_in, precision=HIGHEST)
    real_part = cosine_part[:, :, 0] + orient * sine_part[:, :, 1]
    imag_part = cosine_part[:, :, 1] - orient * sine_part[:, :, 0]
    return jnp.stack([real_part, imag_part], axis=2)


def lat_out(values_in, cosine_out, sine_out, orient):
    cosine_part = jnp.einsum("jih,shrmc->jsirmc", cosine_out, values_in, precision=HIGHEST)
    sine_part = jnp.einsum("jih,shrmc->jsirmc", sine_out, values_in, precision=HIGHEST)
    real_part = cosine_part[:, :, :, 0] + orient * sine_part[:, :, :, 1]
    imag_part = cosine_part[:, :, :, 1] - orient * sine_part[:, :, :, 0]
    return jnp.stack([real_part, imag_part], axis=3)


def local(tokens, norm_gain, norm_shift, weight_one, bias_one, weight_two, bias_two, cotangent):
    lat_parts = lax.axis_size("lat")
    samples, local_rows, lon_cells, features = tokens.shape
    groups = weight_one.shape[1]
    block_size = weight_one.shape[2]
    lat_rows = local_rows * lat_parts
    kept_modes = lon_cells // 2 + 1
    padded = (kept_modes + lat_parts - 1) // lat_parts * lat_parts
    local_modes = padded // lat_parts
    lon_table = lon_basis(lon_cells, padded)
    weighted = lon_table * lon_weight(lon_cells, padded)[None, None, :]
    lon_blocks = lon_table.reshape(lon_cells, 2, lat_parts, local_modes)
    weighted_blocks = weighted.reshape(lon_cells, 2, lat_parts, local_modes)
    cosine, sine_table = lat_basis(lat_rows)
    cosine_in = cosine.reshape(lat_rows, lat_parts, local_rows)
    sine_in = sine_table.reshape(lat_rows, lat_parts, local_rows)
    cosine_out = cosine.reshape(lat_parts, local_rows, lat_rows)
    sine_out = sine_table.reshape(lat_parts, local_rows, lat_rows)
    float_tokens = tokens.astype(jnp.float32)
    average = jnp.mean(float_tokens, axis=-1, keepdims=True)
    centred = float_tokens - average
    variance = jnp.mean(centred * centred, axis=-1, keepdims=True)
    inverse_std = lax.rsqrt(variance + EPSILON)
    normalized = centred * inverse_std
    normed = normalized * norm_gain + norm_shift
    upstream_out = cotangent.astype(jnp.float32)
    lon_spectrum = jnp.einsum("shwc,wrjm->jshrmc", normed, lon_blocks, precision=HIGHEST)
    cotangent_lon = jnp.einsum("shwc,wrjm->jshrmc", upstream_out, weighted_blocks, precision=HIGHEST)
    leaving_modes = jnp.concatenate([lon_spectrum, cotangent_lon], axis=3)
    arrived = lax.all_to_all(leaving_modes, "lat", 0, 0, tiled=True)
    mode_shape = (samples, lat_rows, 2, local_modes, groups, block_size)
    row_shape = (samples, lat_rows, 2, local_modes, features)
    spectrum = lat_in(arrived[:, :, :, :2], cosine_in, sine_in, 1.0).reshape(mode_shape)
    pre_inner = block_product(spectrum, weight_one) + bias_one[None, None, :, None]
    inner_act, gelu_back = jax.vjp(jax.nn.gelu, pre_inner)
    pre_outer = block_product(inner_act, weight_two) + bias_two[None, None, :, None]
    shrunk, shrink_back = jax.vjp(shrink, pre_outer)
    leaving = lat_out(shrunk.reshape(row_shape), cosine_out, sine_out, -1.0)
    shrunk_grad = lat_in(arrived[:, :, :, 2:], cosine_in, sine_in, 1.0).reshape(mode_shape)
    outer_grad = shrink_back(shrunk_grad)[0]
    weight_two_grad = weight_grad(inner_act, outer_grad)
    bias_two_grad = jnp.sum(outer_grad, axis=(0, 1, 3))
    inner_grad = gelu_back(block_adjoint(outer_grad, weight_two))[0]
    weight_one_grad = weight_grad(spectrum, inner_grad)
    bias_one_grad = jnp.sum(inner_grad, axis=(0, 1, 3))
    spectrum_grad = block_adjoint(inner_grad, weight_one).reshape(row_shape)
    adjoint_modes = lat_out(spectrum_grad, cosine_out, sine_out, -1.0)
    leaving_rows = jnp.concatenate([leaving, adjoint_modes], axis=3)
    returned = lax.all_to_all(leaving_rows, "lat", 0, 0, tiled=True)
    filtered = jnp.einsum(
        "jshrmc,wrjm->shwc", returned[:, :, :, :2], weighted_blocks, precision=HIGHEST
    )
    block_out = (float_tokens + normed + filtered).astype(jnp.bfloat16)
    normed_grad = upstream_out + jnp.einsum(
        "jshrmc,wrjm->shwc", returned[:, :, :, 2:], lon_blocks, precision=HIGHEST
    )
    hat_grad = normed_grad * norm_gain
    hat_mean = jnp.mean(hat_grad, axis=-1, keepdims=True)
    cross_mean = jnp.mean(hat_grad * normalized, axis=-1, keepdims=True)
    grad_input = upstream_out + inverse_std * (hat_grad - hat_mean - normalized * cross_mean)
    local_gain = jnp.sum(normed_grad * normalized, axis=(0, 1, 2))
    local_shift = jnp.sum(normed_grad, axis=(0, 1, 2))
    summed = flat_sum(
        (
            weight_one_grad,
            bias_one_grad,
            weight_two_grad,
            bias_two_grad,
            local_gain,
            local_shift,
        ),
        ("sample", "lat"),
    )
    return (
        block_out,
        grad_input.astype(jnp.bfloat16),
        summed[4],
        summed[5],
        summed[0],
        summed[1],
        summed[2],
        summed[3],
    )


def solution(mesh):
    placed = (
        P("sample", "lat", None, None),
        P(),
        P(),
        P(),
        P(),
        P(),
        P(),
        P("sample", "lat", None, None),
    )
    return jax.shard_map(
        local,
        mesh=mesh,
        in_specs=placed,
        out_specs=(
            P("sample", "lat", None, None),
            P("sample", "lat", None, None),
            P(),
            P(),
            P(),
            P(),
            P(),
            P(),
        ),
        check_vma=False,
    )
```

```python
import jax
import jax.numpy as jnp
from jax import lax
from jax.sharding import PartitionSpec as P

HIGHEST = lax.Precision.HIGHEST
SHRINK = 0.01
EPSILON = 1e-05


def lon_basis(cell_count, mode_count):
    cell_index = jnp.arange(cell_count, dtype=jnp.int32)[:, None]
    mode_index = jnp.arange(mode_count, dtype=jnp.int32)[None, :]
    phase_int = (cell_index * mode_index % cell_count).astype(jnp.float32)
    phase_angle = phase_int * (2.0 * jnp.pi / cell_count)
    keep_scale = (mode_index < cell_count // 2 + 1).astype(jnp.float32) / jnp.sqrt(
        jnp.float32(cell_count)
    )
    return jnp.stack(
        [jnp.cos(phase_angle) * keep_scale, -jnp.sin(phase_angle) * keep_scale], axis=1
    )


def lon_weight(cell_count, mode_count):
    mode_index = jnp.arange(mode_count, dtype=jnp.int32)
    single = jnp.logical_or(mode_index == 0, 2 * mode_index == cell_count)
    return jnp.where(single, 1.0, 2.0).astype(jnp.float32)


def lat_basis(row_count):
    row_index = jnp.arange(row_count, dtype=jnp.int32)
    phase_int = (row_index[:, None] * row_index[None, :] % row_count).astype(jnp.float32)
    phase_angle = phase_int * (2.0 * jnp.pi / row_count)
    norm_factor = 1.0 / jnp.sqrt(jnp.float32(row_count))
    return (jnp.cos(phase_angle) * norm_factor, jnp.sin(phase_angle) * norm_factor)


def lat_apply(values_in, cosine, sine_table, orient):
    cosine_part = jnp.einsum("ph,shrkc->sprkc", cosine, values_in, precision=HIGHEST)
    sine_part = jnp.einsum("ph,shrkc->sprkc", sine_table, values_in, precision=HIGHEST)
    real_part = cosine_part[:, :, 0] + orient * sine_part[:, :, 1]
    imag_part = cosine_part[:, :, 1] - orient * sine_part[:, :, 0]
    return jnp.stack([real_part, imag_part], axis=2)


def block_product(values_in, weights):

    def product_part(part_in, slot_index):
        return jnp.einsum("shkgi,gio->shkgo", part_in, weights[slot_index], precision=HIGHEST)

    real_input = values_in[:, :, 0]
    imag_input = values_in[:, :, 1]
    real_out = product_part(real_input, 0) - product_part(imag_input, 1)
    imag_out = product_part(imag_input, 0) + product_part(real_input, 1)
    return jnp.stack([real_out, imag_out], axis=2)


def block_adjoint(values_in, weights):

    def product_part(part_in, slot_index):
        return jnp.einsum("shkgo,gio->shkgi", part_in, weights[slot_index], precision=HIGHEST)

    real_input = values_in[:, :, 0]
    imag_input = values_in[:, :, 1]
    real_out = product_part(real_input, 0) + product_part(imag_input, 1)
    imag_out = product_part(imag_input, 0) - product_part(real_input, 1)
    return jnp.stack([real_out, imag_out], axis=2)


def weight_grad(inputs, upstream):

    def contract(left_side, right_side):
        return jnp.einsum("shkgi,shkgo->gio", left_side, right_side, precision=HIGHEST)

    real_input = inputs[:, :, 0]
    imag_input = inputs[:, :, 1]
    real_upper = upstream[:, :, 0]
    imag_upper = upstream[:, :, 1]
    first = contract(real_input, real_upper) + contract(imag_input, imag_upper)
    second = contract(real_input, imag_upper) - contract(imag_input, real_upper)
    return jnp.stack([first, second], axis=0)


def shrink(values):
    return values - SHRINK * values * lax.rsqrt(values * values + SHRINK * SHRINK)


def flat_sum(parts, axes):
    count = 1
    for name in axes:
        count *= lax.axis_size(name)
    flat = jnp.concatenate([part.reshape(-1) for part in parts])
    size = flat.shape[0]
    chunk = -(-size // (count * 128)) * 128
    flat = jnp.pad(flat, (0, count * chunk - size)).reshape(count, chunk)
    reduced = lax.all_to_all(flat, axes, 0, 0, tiled=True).sum(axis=0)
    spread = jnp.broadcast_to(reduced[None], (count, chunk))
    whole = lax.all_to_all(spread, axes, 0, 0, tiled=True).reshape(-1)
    results = []
    offset = 0
    for part in parts:
        results.append(whole[offset : offset + part.size].reshape(part.shape))
        offset += part.size
    return tuple(results)


def lat_in(values_in, cosine_in, sine_in, orient):
    cosine_part = jnp.einsum("pjh,jshmrc->sprmc", cosine_in, values_in, precision=HIGHEST)
    sine_part = jnp.einsum("pjh,jshmrc->sprmc", sine_in, values_in, precision=HIGHEST)
    real_part = cosine_part[:, :, 0] + orient * sine_part[:, :, 1]
    imag_part = cosine_part[:, :, 1] - orient * sine_part[:, :, 0]
    return jnp.stack([real_part, imag_part], axis=2)


def lat_out(values_in, cosine_out, sine_out, orient):
    cosine_part = jnp.einsum("jih,shrmc->jsimrc", cosine_out, values_in, precision=HIGHEST)
    sine_part = jnp.einsum("jih,shrmc->jsimrc", sine_out, values_in, precision=HIGHEST)
    real_part = cosine_part[:, :, :, :, 0] + orient * sine_part[:, :, :, :, 1]
    imag_part = cosine_part[:, :, :, :, 1] - orient * sine_part[:, :, :, :, 0]
    return jnp.stack([real_part, imag_part], axis=4)


def chunk_spectral(arrived, tables, weights):
    cosine_in, sine_in, cosine_out, sine_out = tables
    weight_one, bias_one, weight_two, bias_two = weights
    samples = arrived.shape[1]
    local_modes = arrived.shape[3]
    lat_rows = cosine_in.shape[0]
    groups = weight_one.shape[1]
    block_size = weight_one.shape[2]
    mode_shape = (samples, lat_rows, 2, local_modes, groups, block_size)
    row_shape = (samples, lat_rows, 2, local_modes, groups * block_size)
    spectrum = lat_in(arrived[:, :, :, :, :2], cosine_in, sine_in, 1.0).reshape(mode_shape)
    pre_inner = block_product(spectrum, weight_one) + bias_one[None, None, :, None]
    inner_act, gelu_back = jax.vjp(jax.nn.gelu, pre_inner)
    pre_outer = block_product(inner_act, weight_two) + bias_two[None, None, :, None]
    shrunk, shrink_back = jax.vjp(shrink, pre_outer)
    leaving = lat_out(shrunk.reshape(row_shape), cosine_out, sine_out, -1.0)
    shrunk_grad = lat_in(arrived[:, :, :, :, 2:], cosine_in, sine_in, 1.0).reshape(mode_shape)
    outer_grad = shrink_back(shrunk_grad)[0]
    weight_two_grad = weight_grad(inner_act, outer_grad)
    bias_two_grad = jnp.sum(outer_grad, axis=(0, 1, 3))
    inner_grad = gelu_back(block_adjoint(outer_grad, weight_two))[0]
    weight_one_grad = weight_grad(spectrum, inner_grad)
    bias_one_grad = jnp.sum(inner_grad, axis=(0, 1, 3))
    spectrum_grad = block_adjoint(inner_grad, weight_one).reshape(row_shape)
    adjoint_modes = lat_out(spectrum_grad, cosine_out, sine_out, -1.0)
    leaving_rows = jnp.concatenate([leaving, adjoint_modes], axis=4)
    return leaving_rows, (weight_one_grad, bias_one_grad, weight_two_grad, bias_two_grad)


def local(tokens, norm_gain, norm_shift, weight_one, bias_one, weight_two, bias_two, cotangent):
    lat_parts = lax.axis_size("lat")
    samples, local_rows, lon_cells, features = tokens.shape
    groups = weight_one.shape[1]
    block_size = weight_one.shape[2]
    chunks = 2 if groups % 2 == 0 else 1
    chunk_groups = groups // chunks
    chunk_width = chunk_groups * block_size
    lat_rows = local_rows * lat_parts
    kept_modes = lon_cells // 2 + 1
    padded = (kept_modes + lat_parts - 1) // lat_parts * lat_parts
    local_modes = padded // lat_parts
    lon_table = lon_basis(lon_cells, padded)
    weighted = lon_table * lon_weight(lon_cells, padded)[None, None, :]
    lon_blocks = lon_table.reshape(lon_cells, 2, lat_parts, local_modes)
    weighted_blocks = weighted.reshape(lon_cells, 2, lat_parts, local_modes)
    cosine, sine_table = lat_basis(lat_rows)
    tables = (
        cosine.reshape(lat_rows, lat_parts, local_rows),
        sine_table.reshape(lat_rows, lat_parts, local_rows),
        cosine.reshape(lat_parts, local_rows, lat_rows),
        sine_table.reshape(lat_parts, local_rows, lat_rows),
    )
    float_tokens = tokens.astype(jnp.float32)
    average = jnp.mean(float_tokens, axis=-1, keepdims=True)
    centred = float_tokens - average
    variance = jnp.mean(centred * centred, axis=-1, keepdims=True)
    inverse_std = lax.rsqrt(variance + EPSILON)
    normalized = centred * inverse_std
    normed = normalized * norm_gain + norm_shift
    upstream_out = cotangent.astype(jnp.float32)
    arrivals = []
    for index in range(chunks):
        cut = slice(index * chunk_width, (index + 1) * chunk_width)
        lon_spectrum = jnp.einsum(
            "shwc,wrjm->jshmrc", normed[..., cut], lon_blocks, precision=HIGHEST
        )
        cotangent_lon = jnp.einsum(
            "shwc,wrjm->jshmrc", upstream_out[..., cut], weighted_blocks, precision=HIGHEST
        )
        leaving_modes = jnp.concatenate([lon_spectrum, cotangent_lon], axis=4)
        arrivals.append(lax.all_to_all(leaving_modes, "lat", 0, 0, tiled=True))
    filtered_parts = []
    adjoint_parts = []
    grad_parts = []
    leaving_all = []
    for index in range(chunks):
        part = slice(index * chunk_groups, (index + 1) * chunk_groups)
        weights = (weight_one[:, part], bias_one[:, part], weight_two[:, part], bias_two[:, part])
        arrived = arrivals[index]
        if index > 0:
            arrived, leaving_all[index - 1] = lax.optimization_barrier(
                (arrived, leaving_all[index - 1])
            )
        leaving_rows, chunk_grads = chunk_spectral(arrived, tables, weights)
        leaving_all.append(leaving_rows)
        grad_parts.append(chunk_grads)
    returns = [lax.all_to_all(rows, "lat", 0, 0, tiled=True) for rows in leaving_all]
    for index in range(chunks):
        returned = returns[index]
        if index + 1 < chunks:
            returned, _ = lax.optimization_barrier((returned, leaving_all[index + 1]))
        filtered_parts.append(
            jnp.einsum(
                "jshmrc,wrjm->shwc", returned[:, :, :, :, :2], weighted_blocks, precision=HIGHEST
            )
        )
        adjoint_parts.append(
            jnp.einsum("jshmrc,wrjm->shwc", returned[:, :, :, :, 2:], lon_blocks, precision=HIGHEST)
        )
    local_grads = tuple(
        jnp.concatenate([grads[slot] for grads in grad_parts], axis=1) for slot in range(4)
    )
    local_grads, _ = lax.optimization_barrier((local_grads, returns[-1]))
    spectral_grads = flat_sum(local_grads, ("sample", "lat"))
    filtered = jnp.concatenate(filtered_parts, axis=-1)
    block_out = (float_tokens + normed + filtered).astype(jnp.bfloat16)
    normed_grad = upstream_out + jnp.concatenate(adjoint_parts, axis=-1)
    hat_grad = normed_grad * norm_gain
    hat_mean = jnp.mean(hat_grad, axis=-1, keepdims=True)
    cross_mean = jnp.mean(hat_grad * normalized, axis=-1, keepdims=True)
    grad_input = upstream_out + inverse_std * (hat_grad - hat_mean - normalized * cross_mean)
    local_gain = jnp.sum(normed_grad * normalized, axis=(0, 1, 2))
    local_shift = jnp.sum(normed_grad, axis=(0, 1, 2))
    norm_grads = flat_sum((local_gain, local_shift), ("sample", "lat"))
    return (
        block_out,
        grad_input.astype(jnp.bfloat16),
        norm_grads[0],
        norm_grads[1],
        spectral_grads[0],
        spectral_grads[1],
        spectral_grads[2],
        spectral_grads[3],
    )


def solution(mesh):
    placed = (
        P("sample", "lat", None, None),
        P(),
        P(),
        P(),
        P(),
        P(),
        P(),
        P("sample", "lat", None, None),
    )
    return jax.shard_map(
        local,
        mesh=mesh,
        in_specs=placed,
        out_specs=(
            P("sample", "lat", None, None),
            P("sample", "lat", None, None),
            P(),
            P(),
            P(),
            P(),
            P(),
            P(),
        ),
        check_vma=False,
    )
```

```python
import jax
import jax.numpy as jnp
from jax import lax
from jax.sharding import PartitionSpec as P

HIGHEST = lax.Precision.HIGHEST
SHRINK = 0.01
EPSILON = 1e-05


def lon_basis(cell_count, mode_count):
    cell_index = jnp.arange(cell_count, dtype=jnp.int32)[:, None]
    mode_index = jnp.arange(mode_count, dtype=jnp.int32)[None, :]
    phase_int = (cell_index * mode_index % cell_count).astype(jnp.float32)
    phase_angle = phase_int * (2.0 * jnp.pi / cell_count)
    keep_scale = (mode_index < cell_count // 2 + 1).astype(jnp.float32) / jnp.sqrt(
        jnp.float32(cell_count)
    )
    return jnp.stack(
        [jnp.cos(phase_angle) * keep_scale, -jnp.sin(phase_angle) * keep_scale], axis=1
    )


def lon_weight(cell_count, mode_count):
    mode_index = jnp.arange(mode_count, dtype=jnp.int32)
    single = jnp.logical_or(mode_index == 0, 2 * mode_index == cell_count)
    return jnp.where(single, 1.0, 2.0).astype(jnp.float32)


def lat_basis(row_count):
    row_index = jnp.arange(row_count, dtype=jnp.int32)
    phase_int = (row_index[:, None] * row_index[None, :] % row_count).astype(jnp.float32)
    phase_angle = phase_int * (2.0 * jnp.pi / row_count)
    norm_factor = 1.0 / jnp.sqrt(jnp.float32(row_count))
    return (jnp.cos(phase_angle) * norm_factor, jnp.sin(phase_angle) * norm_factor)


def lat_apply(values_in, cosine, sine_table, orient):
    cosine_part = jnp.einsum("ph,shrkc->sprkc", cosine, values_in, precision=HIGHEST)
    sine_part = jnp.einsum("ph,shrkc->sprkc", sine_table, values_in, precision=HIGHEST)
    real_part = cosine_part[:, :, 0] + orient * sine_part[:, :, 1]
    imag_part = cosine_part[:, :, 1] - orient * sine_part[:, :, 0]
    return jnp.stack([real_part, imag_part], axis=2)


def block_product(values_in, weights):

    def product_part(part_in, slot_index):
        return jnp.einsum("shkgi,gio->shkgo", part_in, weights[slot_index], precision=HIGHEST)

    real_input = values_in[:, :, 0]
    imag_input = values_in[:, :, 1]
    real_out = product_part(real_input, 0) - product_part(imag_input, 1)
    imag_out = product_part(imag_input, 0) + product_part(real_input, 1)
    return jnp.stack([real_out, imag_out], axis=2)


def block_adjoint(values_in, weights):

    def product_part(part_in, slot_index):
        return jnp.einsum("shkgo,gio->shkgi", part_in, weights[slot_index], precision=HIGHEST)

    real_input = values_in[:, :, 0]
    imag_input = values_in[:, :, 1]
    real_out = product_part(real_input, 0) + product_part(imag_input, 1)
    imag_out = product_part(imag_input, 0) - product_part(real_input, 1)
    return jnp.stack([real_out, imag_out], axis=2)


def weight_grad(inputs, upstream):

    def contract(left_side, right_side):
        return jnp.einsum("shkgi,shkgo->gio", left_side, right_side, precision=HIGHEST)

    real_input = inputs[:, :, 0]
    imag_input = inputs[:, :, 1]
    real_upper = upstream[:, :, 0]
    imag_upper = upstream[:, :, 1]
    first = contract(real_input, real_upper) + contract(imag_input, imag_upper)
    second = contract(real_input, imag_upper) - contract(imag_input, real_upper)
    return jnp.stack([first, second], axis=0)


def shrink(values):
    return values - SHRINK * values * lax.rsqrt(values * values + SHRINK * SHRINK)


def flat_sum(parts, axes):
    count = 1
    for name in axes:
        count *= lax.axis_size(name)
    flat = jnp.concatenate([part.reshape(-1) for part in parts])
    size = flat.shape[0]
    chunk = -(-size // (count * 128)) * 128
    flat = jnp.pad(flat, (0, count * chunk - size)).reshape(count, chunk)
    reduced = lax.all_to_all(flat, axes, 0, 0, tiled=True).sum(axis=0)
    spread = jnp.broadcast_to(reduced[None], (count, chunk))
    whole = lax.all_to_all(spread, axes, 0, 0, tiled=True).reshape(-1)
    results = []
    offset = 0
    for part in parts:
        results.append(whole[offset : offset + part.size].reshape(part.shape))
        offset += part.size
    return tuple(results)


def lat_in(values_in, cosine_in, sine_in, orient):
    cosine_part = jnp.einsum("pjh,jshmrc->sprmc", cosine_in, values_in, precision=HIGHEST)
    sine_part = jnp.einsum("pjh,jshmrc->sprmc", sine_in, values_in, precision=HIGHEST)
    real_part = cosine_part[:, :, 0] + orient * sine_part[:, :, 1]
    imag_part = cosine_part[:, :, 1] - orient * sine_part[:, :, 0]
    return jnp.stack([real_part, imag_part], axis=2)


def lat_out(values_in, cosine_out, sine_out, orient):
    cosine_part = jnp.einsum("jih,shrmc->jsimrc", cosine_out, values_in, precision=HIGHEST)
    sine_part = jnp.einsum("jih,shrmc->jsimrc", sine_out, values_in, precision=HIGHEST)
    real_part = cosine_part[:, :, :, :, 0] + orient * sine_part[:, :, :, :, 1]
    imag_part = cosine_part[:, :, :, :, 1] - orient * sine_part[:, :, :, :, 0]
    return jnp.stack([real_part, imag_part], axis=4)


def chunk_spectral(arrived, tables, weights):
    cosine_in, sine_in, cosine_out, sine_out = tables
    weight_one, bias_one, weight_two, bias_two = weights
    samples = arrived.shape[1]
    local_modes = arrived.shape[3]
    lat_rows = cosine_in.shape[0]
    groups = weight_one.shape[1]
    block_size = weight_one.shape[2]
    mode_shape = (samples, lat_rows, 2, local_modes, groups, block_size)
    row_shape = (samples, lat_rows, 2, local_modes, groups * block_size)
    spectrum = lat_in(arrived[:, :, :, :, :2], cosine_in, sine_in, 1.0).reshape(mode_shape)
    pre_inner = block_product(spectrum, weight_one) + bias_one[None, None, :, None]
    inner_act, gelu_back = jax.vjp(jax.nn.gelu, pre_inner)
    pre_outer = block_product(inner_act, weight_two) + bias_two[None, None, :, None]
    shrunk, shrink_back = jax.vjp(shrink, pre_outer)
    leaving = lat_out(shrunk.reshape(row_shape), cosine_out, sine_out, -1.0)
    shrunk_grad = lat_in(arrived[:, :, :, :, 2:], cosine_in, sine_in, 1.0).reshape(mode_shape)
    outer_grad = shrink_back(shrunk_grad)[0]
    weight_two_grad = weight_grad(inner_act, outer_grad)
    bias_two_grad = jnp.sum(outer_grad, axis=(0, 1, 3))
    inner_grad = gelu_back(block_adjoint(outer_grad, weight_two))[0]
    weight_one_grad = weight_grad(spectrum, inner_grad)
    bias_one_grad = jnp.sum(inner_grad, axis=(0, 1, 3))
    spectrum_grad = block_adjoint(inner_grad, weight_one).reshape(row_shape)
    adjoint_modes = lat_out(spectrum_grad, cosine_out, sine_out, -1.0)
    leaving_rows = jnp.concatenate([leaving, adjoint_modes], axis=4)
    return leaving_rows, (weight_one_grad, bias_one_grad, weight_two_grad, bias_two_grad)


def local(tokens, norm_gain, norm_shift, weight_one, bias_one, weight_two, bias_two, cotangent):
    lat_parts = lax.axis_size("lat")
    samples, local_rows, lon_cells, features = tokens.shape
    groups = weight_one.shape[1]
    block_size = weight_one.shape[2]
    chunks = 2 if groups % 2 == 0 else 1
    chunk_groups = groups // chunks
    chunk_width = chunk_groups * block_size
    lat_rows = local_rows * lat_parts
    kept_modes = lon_cells // 2 + 1
    padded = (kept_modes + lat_parts - 1) // lat_parts * lat_parts
    local_modes = padded // lat_parts
    lon_table = lon_basis(lon_cells, padded)
    weighted = lon_table * lon_weight(lon_cells, padded)[None, None, :]
    lon_blocks = lon_table.reshape(lon_cells, 2, lat_parts, local_modes)
    weighted_blocks = weighted.reshape(lon_cells, 2, lat_parts, local_modes)
    cosine, sine_table = lat_basis(lat_rows)
    tables = (
        cosine.reshape(lat_rows, lat_parts, local_rows),
        sine_table.reshape(lat_rows, lat_parts, local_rows),
        cosine.reshape(lat_parts, local_rows, lat_rows),
        sine_table.reshape(lat_parts, local_rows, lat_rows),
    )
    float_tokens = tokens.astype(jnp.float32)
    average = jnp.mean(float_tokens, axis=-1, keepdims=True)
    centred = float_tokens - average
    variance = jnp.mean(centred * centred, axis=-1, keepdims=True)
    inverse_std = lax.rsqrt(variance + EPSILON)
    normalized = centred * inverse_std
    normed = normalized * norm_gain + norm_shift
    upstream_out = cotangent.astype(jnp.float32)
    arrivals = []
    for index in range(chunks):
        cut = slice(index * chunk_width, (index + 1) * chunk_width)
        lon_spectrum = jnp.einsum(
            "shwc,wrjm->jshmrc", normed[..., cut], lon_blocks, precision=HIGHEST
        )
        cotangent_lon = jnp.einsum(
            "shwc,wrjm->jshmrc", upstream_out[..., cut], weighted_blocks, precision=HIGHEST
        )
        leaving_modes = jnp.concatenate([lon_spectrum, cotangent_lon], axis=4)
        arrivals.append(lax.all_to_all(leaving_modes, "lat", 0, 0, tiled=True))
    filtered_parts = []
    adjoint_parts = []
    grad_parts = []
    leaving_all = []
    for index in range(chunks):
        part = slice(index * chunk_groups, (index + 1) * chunk_groups)
        weights = (weight_one[:, part], bias_one[:, part], weight_two[:, part], bias_two[:, part])
        arrived = arrivals[index]
        if index > 0:
            arrived, leaving_all[index - 1] = lax.optimization_barrier(
                (arrived, leaving_all[index - 1])
            )
        leaving_rows, chunk_grads = chunk_spectral(arrived, tables, weights)
        leaving_all.append(leaving_rows)
        grad_parts.append(chunk_grads)
    returns = [lax.all_to_all(rows, "lat", 0, 0, tiled=True) for rows in leaving_all]
    for index in range(chunks):
        returned = returns[index]
        if index + 1 < chunks:
            returned, _ = lax.optimization_barrier((returned, leaving_all[index + 1]))
        filtered_parts.append(
            jnp.einsum(
                "jshmrc,wrjm->shwc", returned[:, :, :, :, :2], weighted_blocks, precision=HIGHEST
            )
        )
        adjoint_parts.append(
            jnp.einsum("jshmrc,wrjm->shwc", returned[:, :, :, :, 2:], lon_blocks, precision=HIGHEST)
        )
    local_grads = tuple(
        jnp.concatenate([grads[slot] for grads in grad_parts], axis=1) for slot in range(4)
    )
    filtered = jnp.concatenate(filtered_parts, axis=-1)
    block_out = (float_tokens + normed + filtered).astype(jnp.bfloat16)
    normed_grad = upstream_out + jnp.concatenate(adjoint_parts, axis=-1)
    hat_grad = normed_grad * norm_gain
    hat_mean = jnp.mean(hat_grad, axis=-1, keepdims=True)
    cross_mean = jnp.mean(hat_grad * normalized, axis=-1, keepdims=True)
    grad_input = upstream_out + inverse_std * (hat_grad - hat_mean - normalized * cross_mean)
    local_gain = jnp.sum(normed_grad * normalized, axis=(0, 1, 2))
    local_shift = jnp.sum(normed_grad, axis=(0, 1, 2))
    summed = flat_sum(local_grads + (local_gain, local_shift), ("sample", "lat"))
    spectral_grads = summed[:4]
    norm_grads = summed[4:]
    return (
        block_out,
        grad_input.astype(jnp.bfloat16),
        norm_grads[0],
        norm_grads[1],
        spectral_grads[0],
        spectral_grads[1],
        spectral_grads[2],
        spectral_grads[3],
    )


def solution(mesh):
    placed = (
        P("sample", "lat", None, None),
        P(),
        P(),
        P(),
        P(),
        P(),
        P(),
        P("sample", "lat", None, None),
    )
    return jax.shard_map(
        local,
        mesh=mesh,
        in_specs=placed,
        out_specs=(
            P("sample", "lat", None, None),
            P("sample", "lat", None, None),
            P(),
            P(),
            P(),
            P(),
            P(),
            P(),
        ),
        check_vma=False,
    )
```

```python
import jax
import jax.numpy as jnp
from jax import lax
from jax.sharding import PartitionSpec as P

HIGHEST = lax.Precision.HIGHEST
SHRINK = 0.01
EPSILON = 1e-05


def lon_basis(cell_count, mode_count):
    cell_index = jnp.arange(cell_count, dtype=jnp.int32)[:, None]
    mode_index = jnp.arange(mode_count, dtype=jnp.int32)[None, :]
    phase_int = (cell_index * mode_index % cell_count).astype(jnp.float32)
    phase_angle = phase_int * (2.0 * jnp.pi / cell_count)
    keep_scale = (mode_index < cell_count // 2 + 1).astype(jnp.float32) / jnp.sqrt(
        jnp.float32(cell_count)
    )
    return jnp.stack(
        [jnp.cos(phase_angle) * keep_scale, -jnp.sin(phase_angle) * keep_scale], axis=1
    )


def lon_weight(cell_count, mode_count):
    mode_index = jnp.arange(mode_count, dtype=jnp.int32)
    single = jnp.logical_or(mode_index == 0, 2 * mode_index == cell_count)
    return jnp.where(single, 1.0, 2.0).astype(jnp.float32)


def lat_basis(row_count):
    row_index = jnp.arange(row_count, dtype=jnp.int32)
    phase_int = (row_index[:, None] * row_index[None, :] % row_count).astype(jnp.float32)
    phase_angle = phase_int * (2.0 * jnp.pi / row_count)
    norm_factor = 1.0 / jnp.sqrt(jnp.float32(row_count))
    return (jnp.cos(phase_angle) * norm_factor, jnp.sin(phase_angle) * norm_factor)


def lat_apply(values_in, cosine, sine_table, orient):
    cosine_part = jnp.einsum("ph,shrkc->sprkc", cosine, values_in, precision=HIGHEST)
    sine_part = jnp.einsum("ph,shrkc->sprkc", sine_table, values_in, precision=HIGHEST)
    real_part = cosine_part[:, :, 0] + orient * sine_part[:, :, 1]
    imag_part = cosine_part[:, :, 1] - orient * sine_part[:, :, 0]
    return jnp.stack([real_part, imag_part], axis=2)


def block_product(values_in, weights):

    def product_part(part_in, slot_index):
        return jnp.einsum("shkgi,gio->shkgo", part_in, weights[slot_index], precision=HIGHEST)

    real_input = values_in[:, :, 0]
    imag_input = values_in[:, :, 1]
    real_out = product_part(real_input, 0) - product_part(imag_input, 1)
    imag_out = product_part(imag_input, 0) + product_part(real_input, 1)
    return jnp.stack([real_out, imag_out], axis=2)


def block_adjoint(values_in, weights):

    def product_part(part_in, slot_index):
        return jnp.einsum("shkgo,gio->shkgi", part_in, weights[slot_index], precision=HIGHEST)

    real_input = values_in[:, :, 0]
    imag_input = values_in[:, :, 1]
    real_out = product_part(real_input, 0) + product_part(imag_input, 1)
    imag_out = product_part(imag_input, 0) - product_part(real_input, 1)
    return jnp.stack([real_out, imag_out], axis=2)


def weight_grad(inputs, upstream):

    def contract(left_side, right_side):
        return jnp.einsum("shkgi,shkgo->gio", left_side, right_side, precision=HIGHEST)

    real_input = inputs[:, :, 0]
    imag_input = inputs[:, :, 1]
    real_upper = upstream[:, :, 0]
    imag_upper = upstream[:, :, 1]
    first = contract(real_input, real_upper) + contract(imag_input, imag_upper)
    second = contract(real_input, imag_upper) - contract(imag_input, real_upper)
    return jnp.stack([first, second], axis=0)


def shrink(values):
    return values - SHRINK * values * lax.rsqrt(values * values + SHRINK * SHRINK)


def flat_sum(parts, axes):
    count = 1
    for name in axes:
        count *= lax.axis_size(name)
    flat = jnp.concatenate([part.reshape(-1) for part in parts])
    size = flat.shape[0]
    chunk = -(-size // (count * 128)) * 128
    flat = jnp.pad(flat, (0, count * chunk - size)).reshape(count, chunk)
    reduced = lax.all_to_all(flat, axes, 0, 0, tiled=True).sum(axis=0)
    spread = jnp.broadcast_to(reduced[None], (count, chunk))
    whole = lax.all_to_all(spread, axes, 0, 0, tiled=True).reshape(-1)
    results = []
    offset = 0
    for part in parts:
        results.append(whole[offset : offset + part.size].reshape(part.shape))
        offset += part.size
    return tuple(results)


def lat_in(values_in, cosine_in, sine_in, orient):
    cosine_part = jnp.einsum("pjh,jshmrc->sprmc", cosine_in, values_in, precision=HIGHEST)
    sine_part = jnp.einsum("pjh,jshmrc->sprmc", sine_in, values_in, precision=HIGHEST)
    real_part = cosine_part[:, :, 0] + orient * sine_part[:, :, 1]
    imag_part = cosine_part[:, :, 1] - orient * sine_part[:, :, 0]
    return jnp.stack([real_part, imag_part], axis=2)


def lat_out(values_in, cosine_out, sine_out, orient):
    cosine_part = jnp.einsum("jih,shrmc->jsimrc", cosine_out, values_in, precision=HIGHEST)
    sine_part = jnp.einsum("jih,shrmc->jsimrc", sine_out, values_in, precision=HIGHEST)
    real_part = cosine_part[:, :, :, :, 0] + orient * sine_part[:, :, :, :, 1]
    imag_part = cosine_part[:, :, :, :, 1] - orient * sine_part[:, :, :, :, 0]
    return jnp.stack([real_part, imag_part], axis=4)


def chunk_spectral(arrived, tables, weights):
    cosine_in, sine_in, cosine_out, sine_out = tables
    weight_one, bias_one, weight_two, bias_two = weights
    samples = arrived.shape[1]
    local_modes = arrived.shape[3]
    lat_rows = cosine_in.shape[0]
    groups = weight_one.shape[1]
    block_size = weight_one.shape[2]
    mode_shape = (samples, lat_rows, 2, local_modes, groups, block_size)
    row_shape = (samples, lat_rows, 2, local_modes, groups * block_size)
    spectrum = lat_in(arrived[:, :, :, :, :2], cosine_in, sine_in, 1.0).reshape(mode_shape)
    pre_inner = block_product(spectrum, weight_one) + bias_one[None, None, :, None]
    inner_act, gelu_back = jax.vjp(jax.nn.gelu, pre_inner)
    pre_outer = block_product(inner_act, weight_two) + bias_two[None, None, :, None]
    shrunk, shrink_back = jax.vjp(shrink, pre_outer)
    leaving = lat_out(shrunk.reshape(row_shape), cosine_out, sine_out, -1.0)
    shrunk_grad = lat_in(arrived[:, :, :, :, 2:], cosine_in, sine_in, 1.0).reshape(mode_shape)
    outer_grad = shrink_back(shrunk_grad)[0]
    weight_two_grad = weight_grad(inner_act, outer_grad)
    bias_two_grad = jnp.sum(outer_grad, axis=(0, 1, 3))
    inner_grad = gelu_back(block_adjoint(outer_grad, weight_two))[0]
    weight_one_grad = weight_grad(spectrum, inner_grad)
    bias_one_grad = jnp.sum(inner_grad, axis=(0, 1, 3))
    spectrum_grad = block_adjoint(inner_grad, weight_one).reshape(row_shape)
    adjoint_modes = lat_out(spectrum_grad, cosine_out, sine_out, -1.0)
    leaving_rows = jnp.concatenate([leaving, adjoint_modes], axis=4)
    return leaving_rows, (weight_one_grad, bias_one_grad, weight_two_grad, bias_two_grad)


def local(tokens, norm_gain, norm_shift, weight_one, bias_one, weight_two, bias_two, cotangent):
    lat_parts = lax.axis_size("lat")
    samples, local_rows, lon_cells, features = tokens.shape
    groups = weight_one.shape[1]
    block_size = weight_one.shape[2]
    chunks = 4 if groups % 4 == 0 else 1
    chunk_groups = groups // chunks
    chunk_width = chunk_groups * block_size
    lat_rows = local_rows * lat_parts
    kept_modes = lon_cells // 2 + 1
    padded = (kept_modes + lat_parts - 1) // lat_parts * lat_parts
    local_modes = padded // lat_parts
    lon_table = lon_basis(lon_cells, padded)
    weighted = lon_table * lon_weight(lon_cells, padded)[None, None, :]
    lon_blocks = lon_table.reshape(lon_cells, 2, lat_parts, local_modes)
    weighted_blocks = weighted.reshape(lon_cells, 2, lat_parts, local_modes)
    cosine, sine_table = lat_basis(lat_rows)
    tables = (
        cosine.reshape(lat_rows, lat_parts, local_rows),
        sine_table.reshape(lat_rows, lat_parts, local_rows),
        cosine.reshape(lat_parts, local_rows, lat_rows),
        sine_table.reshape(lat_parts, local_rows, lat_rows),
    )
    float_tokens = tokens.astype(jnp.float32)
    average = jnp.mean(float_tokens, axis=-1, keepdims=True)
    centred = float_tokens - average
    variance = jnp.mean(centred * centred, axis=-1, keepdims=True)
    inverse_std = lax.rsqrt(variance + EPSILON)
    normalized = centred * inverse_std
    normed = normalized * norm_gain + norm_shift
    upstream_out = cotangent.astype(jnp.float32)
    arrivals = []
    for index in range(chunks):
        cut = slice(index * chunk_width, (index + 1) * chunk_width)
        lon_spectrum = jnp.einsum(
            "shwc,wrjm->jshmrc", normed[..., cut], lon_blocks, precision=HIGHEST
        )
        cotangent_lon = jnp.einsum(
            "shwc,wrjm->jshmrc", upstream_out[..., cut], weighted_blocks, precision=HIGHEST
        )
        leaving_modes = jnp.concatenate([lon_spectrum, cotangent_lon], axis=4)
        arrivals.append(lax.all_to_all(leaving_modes, "lat", 0, 0, tiled=True))
    filtered_parts = []
    adjoint_parts = []
    grad_parts = []
    leaving_all = []
    for index in range(chunks):
        part = slice(index * chunk_groups, (index + 1) * chunk_groups)
        weights = (weight_one[:, part], bias_one[:, part], weight_two[:, part], bias_two[:, part])
        arrived = arrivals[index]
        if index > 0:
            arrived, leaving_all[index - 1] = lax.optimization_barrier(
                (arrived, leaving_all[index - 1])
            )
        leaving_rows, chunk_grads = chunk_spectral(arrived, tables, weights)
        leaving_all.append(leaving_rows)
        grad_parts.append(chunk_grads)
    returns = [lax.all_to_all(rows, "lat", 0, 0, tiled=True) for rows in leaving_all]
    for index in range(chunks):
        returned = returns[index]
        if index + 1 < chunks:
            returned, _ = lax.optimization_barrier((returned, leaving_all[index + 1]))
        filtered_parts.append(
            jnp.einsum(
                "jshmrc,wrjm->shwc", returned[:, :, :, :, :2], weighted_blocks, precision=HIGHEST
            )
        )
        adjoint_parts.append(
            jnp.einsum("jshmrc,wrjm->shwc", returned[:, :, :, :, 2:], lon_blocks, precision=HIGHEST)
        )
    local_grads = tuple(
        jnp.concatenate([grads[slot] for grads in grad_parts], axis=1) for slot in range(4)
    )
    filtered = jnp.concatenate(filtered_parts, axis=-1)
    block_out = (float_tokens + normed + filtered).astype(jnp.bfloat16)
    normed_grad = upstream_out + jnp.concatenate(adjoint_parts, axis=-1)
    hat_grad = normed_grad * norm_gain
    hat_mean = jnp.mean(hat_grad, axis=-1, keepdims=True)
    cross_mean = jnp.mean(hat_grad * normalized, axis=-1, keepdims=True)
    grad_input = upstream_out + inverse_std * (hat_grad - hat_mean - normalized * cross_mean)
    local_gain = jnp.sum(normed_grad * normalized, axis=(0, 1, 2))
    local_shift = jnp.sum(normed_grad, axis=(0, 1, 2))
    summed = flat_sum(local_grads + (local_gain, local_shift), ("sample", "lat"))
    spectral_grads = summed[:4]
    norm_grads = summed[4:]
    return (
        block_out,
        grad_input.astype(jnp.bfloat16),
        norm_grads[0],
        norm_grads[1],
        spectral_grads[0],
        spectral_grads[1],
        spectral_grads[2],
        spectral_grads[3],
    )


def solution(mesh):
    placed = (
        P("sample", "lat", None, None),
        P(),
        P(),
        P(),
        P(),
        P(),
        P(),
        P("sample", "lat", None, None),
    )
    return jax.shard_map(
        local,
        mesh=mesh,
        in_specs=placed,
        out_specs=(
            P("sample", "lat", None, None),
            P("sample", "lat", None, None),
            P(),
            P(),
            P(),
            P(),
            P(),
            P(),
        ),
        check_vma=False,
    )
```

```python
import jax
import jax.numpy as jnp
from jax import lax
from jax.sharding import PartitionSpec as P

HIGHEST = lax.Precision.HIGHEST
SHRINK = 0.01
EPSILON = 1e-05


def lon_basis(cell_count, mode_count):
    cell_index = jnp.arange(cell_count, dtype=jnp.int32)[:, None]
    mode_index = jnp.arange(mode_count, dtype=jnp.int32)[None, :]
    phase_int = (cell_index * mode_index % cell_count).astype(jnp.float32)
    phase_angle = phase_int * (2.0 * jnp.pi / cell_count)
    keep_scale = (mode_index < cell_count // 2 + 1).astype(jnp.float32) / jnp.sqrt(
        jnp.float32(cell_count)
    )
    return jnp.stack(
        [jnp.cos(phase_angle) * keep_scale, -jnp.sin(phase_angle) * keep_scale], axis=1
    )


def lon_weight(cell_count, mode_count):
    mode_index = jnp.arange(mode_count, dtype=jnp.int32)
    single = jnp.logical_or(mode_index == 0, 2 * mode_index == cell_count)
    return jnp.where(single, 1.0, 2.0).astype(jnp.float32)


def lat_basis(row_count):
    row_index = jnp.arange(row_count, dtype=jnp.int32)
    phase_int = (row_index[:, None] * row_index[None, :] % row_count).astype(jnp.float32)
    phase_angle = phase_int * (2.0 * jnp.pi / row_count)
    norm_factor = 1.0 / jnp.sqrt(jnp.float32(row_count))
    return (jnp.cos(phase_angle) * norm_factor, jnp.sin(phase_angle) * norm_factor)


def lat_apply(values_in, cosine, sine_table, orient):
    cosine_part = jnp.einsum("ph,shrkc->sprkc", cosine, values_in, precision=HIGHEST)
    sine_part = jnp.einsum("ph,shrkc->sprkc", sine_table, values_in, precision=HIGHEST)
    real_part = cosine_part[:, :, 0] + orient * sine_part[:, :, 1]
    imag_part = cosine_part[:, :, 1] - orient * sine_part[:, :, 0]
    return jnp.stack([real_part, imag_part], axis=2)


def block_product(values_in, weights):

    def product_part(part_in, slot_index):
        return jnp.einsum("shkgi,gio->shkgo", part_in, weights[slot_index], precision=HIGHEST)

    real_input = values_in[:, :, 0]
    imag_input = values_in[:, :, 1]
    real_out = product_part(real_input, 0) - product_part(imag_input, 1)
    imag_out = product_part(imag_input, 0) + product_part(real_input, 1)
    return jnp.stack([real_out, imag_out], axis=2)


def block_adjoint(values_in, weights):

    def product_part(part_in, slot_index):
        return jnp.einsum("shkgo,gio->shkgi", part_in, weights[slot_index], precision=HIGHEST)

    real_input = values_in[:, :, 0]
    imag_input = values_in[:, :, 1]
    real_out = product_part(real_input, 0) + product_part(imag_input, 1)
    imag_out = product_part(imag_input, 0) - product_part(real_input, 1)
    return jnp.stack([real_out, imag_out], axis=2)


def weight_grad(inputs, upstream):

    def contract(left_side, right_side):
        return jnp.einsum("shkgi,shkgo->gio", left_side, right_side, precision=HIGHEST)

    real_input = inputs[:, :, 0]
    imag_input = inputs[:, :, 1]
    real_upper = upstream[:, :, 0]
    imag_upper = upstream[:, :, 1]
    first = contract(real_input, real_upper) + contract(imag_input, imag_upper)
    second = contract(real_input, imag_upper) - contract(imag_input, real_upper)
    return jnp.stack([first, second], axis=0)


def shrink(values):
    return values - SHRINK * values * lax.rsqrt(values * values + SHRINK * SHRINK)


def flat_sum(parts, axes):
    count = 1
    for name in axes:
        count *= lax.axis_size(name)
    flat = jnp.concatenate([part.reshape(-1) for part in parts])
    size = flat.shape[0]
    chunk = -(-size // (count * 128)) * 128
    flat = jnp.pad(flat, (0, count * chunk - size)).reshape(count, chunk)
    reduced = lax.all_to_all(flat, axes, 0, 0, tiled=True).sum(axis=0)
    spread = jnp.broadcast_to(reduced[None], (count, chunk))
    whole = lax.all_to_all(spread, axes, 0, 0, tiled=True).reshape(-1)
    results = []
    offset = 0
    for part in parts:
        results.append(whole[offset : offset + part.size].reshape(part.shape))
        offset += part.size
    return tuple(results)


def lat_in(values_in, cosine_in, sine_in, orient):
    cosine_part = jnp.einsum("pjh,jshmrc->sprmc", cosine_in, values_in, precision=HIGHEST)
    sine_part = jnp.einsum("pjh,jshmrc->sprmc", sine_in, values_in, precision=HIGHEST)
    real_part = cosine_part[:, :, 0] + orient * sine_part[:, :, 1]
    imag_part = cosine_part[:, :, 1] - orient * sine_part[:, :, 0]
    return jnp.stack([real_part, imag_part], axis=2)


def lat_out(values_in, cosine_out, sine_out, orient):
    cosine_part = jnp.einsum("jih,shrmc->jsimrc", cosine_out, values_in, precision=HIGHEST)
    sine_part = jnp.einsum("jih,shrmc->jsimrc", sine_out, values_in, precision=HIGHEST)
    real_part = cosine_part[:, :, :, :, 0] + orient * sine_part[:, :, :, :, 1]
    imag_part = cosine_part[:, :, :, :, 1] - orient * sine_part[:, :, :, :, 0]
    return jnp.stack([real_part, imag_part], axis=4)


def chunk_spectral(arrived, tables, weights):
    cosine_in, sine_in, cosine_out, sine_out = tables
    weight_one, bias_one, weight_two, bias_two = weights
    samples = arrived.shape[1]
    local_modes = arrived.shape[3]
    lat_rows = cosine_in.shape[0]
    groups = weight_one.shape[1]
    block_size = weight_one.shape[2]
    mode_shape = (samples, lat_rows, 2, local_modes, groups, block_size)
    row_shape = (samples, lat_rows, 2, local_modes, groups * block_size)
    spectrum = lat_in(arrived[:, :, :, :, :2], cosine_in, sine_in, 1.0).reshape(mode_shape)
    pre_inner = block_product(spectrum, weight_one) + bias_one[None, None, :, None]
    inner_act, gelu_back = jax.vjp(jax.nn.gelu, pre_inner)
    pre_outer = block_product(inner_act, weight_two) + bias_two[None, None, :, None]
    shrunk, shrink_back = jax.vjp(shrink, pre_outer)
    leaving = lat_out(shrunk.reshape(row_shape), cosine_out, sine_out, -1.0)
    shrunk_grad = lat_in(arrived[:, :, :, :, 2:], cosine_in, sine_in, 1.0).reshape(mode_shape)
    outer_grad = shrink_back(shrunk_grad)[0]
    weight_two_grad = weight_grad(inner_act, outer_grad)
    bias_two_grad = jnp.sum(outer_grad, axis=(0, 1, 3))
    inner_grad = gelu_back(block_adjoint(outer_grad, weight_two))[0]
    weight_one_grad = weight_grad(spectrum, inner_grad)
    bias_one_grad = jnp.sum(inner_grad, axis=(0, 1, 3))
    spectrum_grad = block_adjoint(inner_grad, weight_one).reshape(row_shape)
    adjoint_modes = lat_out(spectrum_grad, cosine_out, sine_out, -1.0)
    leaving_rows = jnp.concatenate([leaving, adjoint_modes], axis=4)
    return leaving_rows, (weight_one_grad, bias_one_grad, weight_two_grad, bias_two_grad)


def local(tokens, norm_gain, norm_shift, weight_one, bias_one, weight_two, bias_two, cotangent):
    lat_parts = lax.axis_size("lat")
    samples, local_rows, lon_cells, features = tokens.shape
    groups = weight_one.shape[1]
    block_size = weight_one.shape[2]
    bounds = [0, groups * 3 // 8, groups] if groups >= 2 else [0, groups]
    chunks = len(bounds) - 1
    lat_rows = local_rows * lat_parts
    kept_modes = lon_cells // 2 + 1
    padded = (kept_modes + lat_parts - 1) // lat_parts * lat_parts
    local_modes = padded // lat_parts
    lon_table = lon_basis(lon_cells, padded)
    weighted = lon_table * lon_weight(lon_cells, padded)[None, None, :]
    lon_blocks = lon_table.reshape(lon_cells, 2, lat_parts, local_modes)
    weighted_blocks = weighted.reshape(lon_cells, 2, lat_parts, local_modes)
    cosine, sine_table = lat_basis(lat_rows)
    tables = (
        cosine.reshape(lat_rows, lat_parts, local_rows),
        sine_table.reshape(lat_rows, lat_parts, local_rows),
        cosine.reshape(lat_parts, local_rows, lat_rows),
        sine_table.reshape(lat_parts, local_rows, lat_rows),
    )
    float_tokens = tokens.astype(jnp.float32)
    average = jnp.mean(float_tokens, axis=-1, keepdims=True)
    centred = float_tokens - average
    variance = jnp.mean(centred * centred, axis=-1, keepdims=True)
    inverse_std = lax.rsqrt(variance + EPSILON)
    normalized = centred * inverse_std
    normed = normalized * norm_gain + norm_shift
    upstream_out = cotangent.astype(jnp.float32)
    arrivals = []
    for index in range(chunks):
        cut = slice(bounds[index] * block_size, bounds[index + 1] * block_size)
        lon_spectrum = jnp.einsum(
            "shwc,wrjm->jshmrc", normed[..., cut], lon_blocks, precision=HIGHEST
        )
        cotangent_lon = jnp.einsum(
            "shwc,wrjm->jshmrc", upstream_out[..., cut], weighted_blocks, precision=HIGHEST
        )
        leaving_modes = jnp.concatenate([lon_spectrum, cotangent_lon], axis=4)
        arrivals.append(lax.all_to_all(leaving_modes, "lat", 0, 0, tiled=True))
    filtered_parts = []
    adjoint_parts = []
    grad_parts = []
    leaving_all = []
    for index in range(chunks):
        part = slice(bounds[index], bounds[index + 1])
        weights = (weight_one[:, part], bias_one[:, part], weight_two[:, part], bias_two[:, part])
        arrived = arrivals[index]
        if index > 0:
            arrived, leaving_all[index - 1] = lax.optimization_barrier(
                (arrived, leaving_all[index - 1])
            )
        leaving_rows, chunk_grads = chunk_spectral(arrived, tables, weights)
        leaving_all.append(leaving_rows)
        grad_parts.append(chunk_grads)
    returns = [lax.all_to_all(rows, "lat", 0, 0, tiled=True) for rows in leaving_all]
    for index in range(chunks):
        returned = returns[index]
        if index + 1 < chunks:
            returned, _ = lax.optimization_barrier((returned, leaving_all[index + 1]))
        filtered_parts.append(
            jnp.einsum(
                "jshmrc,wrjm->shwc", returned[:, :, :, :, :2], weighted_blocks, precision=HIGHEST
            )
        )
        adjoint_parts.append(
            jnp.einsum("jshmrc,wrjm->shwc", returned[:, :, :, :, 2:], lon_blocks, precision=HIGHEST)
        )
    local_grads = tuple(
        jnp.concatenate([grads[slot] for grads in grad_parts], axis=1) for slot in range(4)
    )
    filtered = jnp.concatenate(filtered_parts, axis=-1)
    block_out = (float_tokens + normed + filtered).astype(jnp.bfloat16)
    normed_grad = upstream_out + jnp.concatenate(adjoint_parts, axis=-1)
    hat_grad = normed_grad * norm_gain
    hat_mean = jnp.mean(hat_grad, axis=-1, keepdims=True)
    cross_mean = jnp.mean(hat_grad * normalized, axis=-1, keepdims=True)
    grad_input = upstream_out + inverse_std * (hat_grad - hat_mean - normalized * cross_mean)
    local_gain = jnp.sum(normed_grad * normalized, axis=(0, 1, 2))
    local_shift = jnp.sum(normed_grad, axis=(0, 1, 2))
    summed = flat_sum(local_grads + (local_gain, local_shift), ("sample", "lat"))
    spectral_grads = summed[:4]
    norm_grads = summed[4:]
    return (
        block_out,
        grad_input.astype(jnp.bfloat16),
        norm_grads[0],
        norm_grads[1],
        spectral_grads[0],
        spectral_grads[1],
        spectral_grads[2],
        spectral_grads[3],
    )


def solution(mesh):
    placed = (
        P("sample", "lat", None, None),
        P(),
        P(),
        P(),
        P(),
        P(),
        P(),
        P("sample", "lat", None, None),
    )
    return jax.shard_map(
        local,
        mesh=mesh,
        in_specs=placed,
        out_specs=(
            P("sample", "lat", None, None),
            P("sample", "lat", None, None),
            P(),
            P(),
            P(),
            P(),
            P(),
            P(),
        ),
        check_vma=False,
    )
```

```python
import jax
import jax.numpy as jnp
from jax import lax
from jax.sharding import PartitionSpec as P

HIGHEST = lax.Precision.HIGHEST
SHRINK = 0.01
EPSILON = 1e-05


def lon_basis(cell_count, mode_count):
    cell_index = jnp.arange(cell_count, dtype=jnp.int32)[:, None]
    mode_index = jnp.arange(mode_count, dtype=jnp.int32)[None, :]
    phase_int = (cell_index * mode_index % cell_count).astype(jnp.float32)
    phase_angle = phase_int * (2.0 * jnp.pi / cell_count)
    keep_scale = (mode_index < cell_count // 2 + 1).astype(jnp.float32) / jnp.sqrt(
        jnp.float32(cell_count)
    )
    return jnp.stack(
        [jnp.cos(phase_angle) * keep_scale, -jnp.sin(phase_angle) * keep_scale], axis=1
    )


def lon_weight(cell_count, mode_count):
    mode_index = jnp.arange(mode_count, dtype=jnp.int32)
    single = jnp.logical_or(mode_index == 0, 2 * mode_index == cell_count)
    return jnp.where(single, 1.0, 2.0).astype(jnp.float32)


def lat_basis(row_count):
    row_index = jnp.arange(row_count, dtype=jnp.int32)
    phase_int = (row_index[:, None] * row_index[None, :] % row_count).astype(jnp.float32)
    phase_angle = phase_int * (2.0 * jnp.pi / row_count)
    norm_factor = 1.0 / jnp.sqrt(jnp.float32(row_count))
    return (jnp.cos(phase_angle) * norm_factor, jnp.sin(phase_angle) * norm_factor)


def lat_apply(values_in, cosine, sine_table, orient):
    cosine_part = jnp.einsum("ph,shrkc->sprkc", cosine, values_in, precision=HIGHEST)
    sine_part = jnp.einsum("ph,shrkc->sprkc", sine_table, values_in, precision=HIGHEST)
    real_part = cosine_part[:, :, 0] + orient * sine_part[:, :, 1]
    imag_part = cosine_part[:, :, 1] - orient * sine_part[:, :, 0]
    return jnp.stack([real_part, imag_part], axis=2)


def block_product(values_in, weights):

    def product_part(part_in, slot_index):
        return jnp.einsum("shkgi,gio->shkgo", part_in, weights[slot_index], precision=HIGHEST)

    real_input = values_in[:, :, 0]
    imag_input = values_in[:, :, 1]
    real_out = product_part(real_input, 0) - product_part(imag_input, 1)
    imag_out = product_part(imag_input, 0) + product_part(real_input, 1)
    return jnp.stack([real_out, imag_out], axis=2)


def block_adjoint(values_in, weights):

    def product_part(part_in, slot_index):
        return jnp.einsum("shkgo,gio->shkgi", part_in, weights[slot_index], precision=HIGHEST)

    real_input = values_in[:, :, 0]
    imag_input = values_in[:, :, 1]
    real_out = product_part(real_input, 0) + product_part(imag_input, 1)
    imag_out = product_part(imag_input, 0) - product_part(real_input, 1)
    return jnp.stack([real_out, imag_out], axis=2)


def weight_grad(inputs, upstream):

    def contract(left_side, right_side):
        return jnp.einsum("shkgi,shkgo->gio", left_side, right_side, precision=HIGHEST)

    real_input = inputs[:, :, 0]
    imag_input = inputs[:, :, 1]
    real_upper = upstream[:, :, 0]
    imag_upper = upstream[:, :, 1]
    first = contract(real_input, real_upper) + contract(imag_input, imag_upper)
    second = contract(real_input, imag_upper) - contract(imag_input, real_upper)
    return jnp.stack([first, second], axis=0)


def shrink(values):
    return values - SHRINK * values * lax.rsqrt(values * values + SHRINK * SHRINK)


def flat_sum(parts, axes):
    count = 1
    for name in axes:
        count *= lax.axis_size(name)
    flat = jnp.concatenate([part.reshape(-1) for part in parts])
    size = flat.shape[0]
    chunk = -(-size // (count * 128)) * 128
    flat = jnp.pad(flat, (0, count * chunk - size)).reshape(count, chunk)
    reduced = lax.all_to_all(flat, axes, 0, 0, tiled=True).sum(axis=0)
    spread = jnp.broadcast_to(reduced[None], (count, chunk))
    whole = lax.all_to_all(spread, axes, 0, 0, tiled=True).reshape(-1)
    results = []
    offset = 0
    for part in parts:
        results.append(whole[offset : offset + part.size].reshape(part.shape))
        offset += part.size
    return tuple(results)


def lat_in(values_in, cosine_in, sine_in, orient):
    cosine_part = jnp.einsum("pjh,jshmrc->sprmc", cosine_in, values_in, precision=HIGHEST)
    sine_part = jnp.einsum("pjh,jshmrc->sprmc", sine_in, values_in, precision=HIGHEST)
    real_part = cosine_part[:, :, 0] + orient * sine_part[:, :, 1]
    imag_part = cosine_part[:, :, 1] - orient * sine_part[:, :, 0]
    return jnp.stack([real_part, imag_part], axis=2)


def lat_out(values_in, cosine_out, sine_out, orient):
    cosine_part = jnp.einsum("jih,shrmc->jsimrc", cosine_out, values_in, precision=HIGHEST)
    sine_part = jnp.einsum("jih,shrmc->jsimrc", sine_out, values_in, precision=HIGHEST)
    real_part = cosine_part[:, :, :, :, 0] + orient * sine_part[:, :, :, :, 1]
    imag_part = cosine_part[:, :, :, :, 1] - orient * sine_part[:, :, :, :, 0]
    return jnp.stack([real_part, imag_part], axis=4)


def chunk_spectral(arrived, tables, weights):
    cosine_in, sine_in, cosine_out, sine_out = tables
    weight_one, bias_one, weight_two, bias_two = weights
    samples = arrived.shape[1]
    local_modes = arrived.shape[3]
    lat_rows = cosine_in.shape[0]
    groups = weight_one.shape[1]
    block_size = weight_one.shape[2]
    mode_shape = (samples, lat_rows, 2, local_modes, groups, block_size)
    row_shape = (samples, lat_rows, 2, local_modes, groups * block_size)
    spectrum = lat_in(arrived[:, :, :, :, :2], cosine_in, sine_in, 1.0).reshape(mode_shape)
    pre_inner = block_product(spectrum, weight_one) + bias_one[None, None, :, None]
    inner_act, gelu_back = jax.vjp(jax.nn.gelu, pre_inner)
    pre_outer = block_product(inner_act, weight_two) + bias_two[None, None, :, None]
    shrunk, shrink_back = jax.vjp(shrink, pre_outer)
    leaving = lat_out(shrunk.reshape(row_shape), cosine_out, sine_out, -1.0)
    shrunk_grad = lat_in(arrived[:, :, :, :, 2:], cosine_in, sine_in, 1.0).reshape(mode_shape)
    outer_grad = shrink_back(shrunk_grad)[0]
    weight_two_grad = weight_grad(inner_act, outer_grad)
    bias_two_grad = jnp.sum(outer_grad, axis=(0, 1, 3))
    inner_grad = gelu_back(block_adjoint(outer_grad, weight_two))[0]
    weight_one_grad = weight_grad(spectrum, inner_grad)
    bias_one_grad = jnp.sum(inner_grad, axis=(0, 1, 3))
    spectrum_grad = block_adjoint(inner_grad, weight_one).reshape(row_shape)
    adjoint_modes = lat_out(spectrum_grad, cosine_out, sine_out, -1.0)
    leaving_rows = jnp.concatenate([leaving, adjoint_modes], axis=4)
    return leaving_rows, (weight_one_grad, bias_one_grad, weight_two_grad, bias_two_grad)


def local(tokens, norm_gain, norm_shift, weight_one, bias_one, weight_two, bias_two, cotangent):
    lat_parts = lax.axis_size("lat")
    samples, local_rows, lon_cells, features = tokens.shape
    groups = weight_one.shape[1]
    block_size = weight_one.shape[2]
    chunks = 2 if groups % 2 == 0 else 1
    chunk_groups = groups // chunks
    chunk_width = chunk_groups * block_size
    lat_rows = local_rows * lat_parts
    kept_modes = lon_cells // 2 + 1
    padded = (kept_modes + lat_parts - 1) // lat_parts * lat_parts
    local_modes = padded // lat_parts
    lon_table = lon_basis(lon_cells, padded)
    weighted = lon_table * lon_weight(lon_cells, padded)[None, None, :]
    lon_blocks = lon_table.reshape(lon_cells, 2, lat_parts, local_modes)
    weighted_blocks = weighted.reshape(lon_cells, 2, lat_parts, local_modes)
    cosine, sine_table = lat_basis(lat_rows)
    tables = (
        cosine.reshape(lat_rows, lat_parts, local_rows),
        sine_table.reshape(lat_rows, lat_parts, local_rows),
        cosine.reshape(lat_parts, local_rows, lat_rows),
        sine_table.reshape(lat_parts, local_rows, lat_rows),
    )
    float_tokens = tokens.astype(jnp.float32)
    average = jnp.mean(float_tokens, axis=-1, keepdims=True)
    centred = float_tokens - average
    variance = jnp.mean(centred * centred, axis=-1, keepdims=True)
    inverse_std = lax.rsqrt(variance + EPSILON)
    normalized = centred * inverse_std
    normed = normalized * norm_gain + norm_shift
    upstream_out = cotangent.astype(jnp.float32)
    arrivals = []
    for index in range(chunks):
        cut = slice(index * chunk_width, (index + 1) * chunk_width)
        lon_spectrum = jnp.einsum(
            "shwc,wrjm->jshmrc", normed[..., cut], lon_blocks, precision=HIGHEST
        )
        cotangent_lon = jnp.einsum(
            "shwc,wrjm->jshmrc", upstream_out[..., cut], weighted_blocks, precision=HIGHEST
        )
        leaving_modes = jnp.concatenate([lon_spectrum, cotangent_lon], axis=4)
        arrivals.append(lax.all_to_all(leaving_modes, "lat", 0, 0, tiled=True))
    filtered_parts = []
    adjoint_parts = []
    grad_parts = []
    leaving_all = []
    for index in range(chunks):
        part = slice(index * chunk_groups, (index + 1) * chunk_groups)
        weights = (weight_one[:, part], bias_one[:, part], weight_two[:, part], bias_two[:, part])
        arrived = arrivals[index]
        if index > 0:
            arrived, leaving_all[index - 1] = lax.optimization_barrier(
                (arrived, leaving_all[index - 1])
            )
        leaving_rows, chunk_grads = chunk_spectral(arrived, tables, weights)
        leaving_all.append(leaving_rows)
        grad_parts.append(chunk_grads)
    returns = [lax.all_to_all(rows, "lat", 0, 0, tiled=True) for rows in leaving_all]
    for index in range(chunks):
        returned = returns[index]
        if index + 1 < chunks:
            returned, _ = lax.optimization_barrier((returned, leaving_all[index + 1]))
        filtered_parts.append(
            jnp.einsum(
                "jshmrc,wrjm->shwc", returned[:, :, :, :, :2], weighted_blocks, precision=HIGHEST
            )
        )
        adjoint_parts.append(
            jnp.einsum("jshmrc,wrjm->shwc", returned[:, :, :, :, 2:], lon_blocks, precision=HIGHEST)
        )
    local_grads = tuple(
        jnp.concatenate([grads[slot] for grads in grad_parts], axis=1) for slot in range(4)
    )
    normed_grad = upstream_out + jnp.concatenate(adjoint_parts, axis=-1)
    hat_grad = normed_grad * norm_gain
    hat_mean = jnp.mean(hat_grad, axis=-1, keepdims=True)
    cross_mean = jnp.mean(hat_grad * normalized, axis=-1, keepdims=True)
    grad_input = upstream_out + inverse_std * (hat_grad - hat_mean - normalized * cross_mean)
    local_gain = jnp.sum(normed_grad * normalized, axis=(0, 1, 2))
    local_shift = jnp.sum(normed_grad, axis=(0, 1, 2))
    summed = flat_sum(local_grads + (local_gain, local_shift), ("sample", "lat"))
    filtered_parts, _ = lax.optimization_barrier((filtered_parts, (local_gain, local_shift)))
    filtered = jnp.concatenate(filtered_parts, axis=-1)
    block_out = (float_tokens + normed + filtered).astype(jnp.bfloat16)
    spectral_grads = summed[:4]
    norm_grads = summed[4:]
    return (
        block_out,
        grad_input.astype(jnp.bfloat16),
        norm_grads[0],
        norm_grads[1],
        spectral_grads[0],
        spectral_grads[1],
        spectral_grads[2],
        spectral_grads[3],
    )


def solution(mesh):
    placed = (
        P("sample", "lat", None, None),
        P(),
        P(),
        P(),
        P(),
        P(),
        P(),
        P("sample", "lat", None, None),
    )
    return jax.shard_map(
        local,
        mesh=mesh,
        in_specs=placed,
        out_specs=(
            P("sample", "lat", None, None),
            P("sample", "lat", None, None),
            P(),
            P(),
            P(),
            P(),
            P(),
            P(),
        ),
        check_vma=False,
    )
```

```python
import jax
import jax.numpy as jnp
from jax import lax
from jax.sharding import PartitionSpec as P

HIGHEST = lax.Precision.HIGHEST
SHRINK = 0.01
EPSILON = 1e-05


def lon_basis(cell_count, mode_count):
    cell_index = jnp.arange(cell_count, dtype=jnp.int32)[:, None]
    mode_index = jnp.arange(mode_count, dtype=jnp.int32)[None, :]
    phase_int = (cell_index * mode_index % cell_count).astype(jnp.float32)
    phase_angle = phase_int * (2.0 * jnp.pi / cell_count)
    keep_scale = (mode_index < cell_count // 2 + 1).astype(jnp.float32) / jnp.sqrt(
        jnp.float32(cell_count)
    )
    return jnp.stack(
        [jnp.cos(phase_angle) * keep_scale, -jnp.sin(phase_angle) * keep_scale], axis=1
    )


def lon_weight(cell_count, mode_count):
    mode_index = jnp.arange(mode_count, dtype=jnp.int32)
    single = jnp.logical_or(mode_index == 0, 2 * mode_index == cell_count)
    return jnp.where(single, 1.0, 2.0).astype(jnp.float32)


def lat_basis(row_count):
    row_index = jnp.arange(row_count, dtype=jnp.int32)
    phase_int = (row_index[:, None] * row_index[None, :] % row_count).astype(jnp.float32)
    phase_angle = phase_int * (2.0 * jnp.pi / row_count)
    norm_factor = 1.0 / jnp.sqrt(jnp.float32(row_count))
    return (jnp.cos(phase_angle) * norm_factor, jnp.sin(phase_angle) * norm_factor)


def lat_apply(values_in, cosine, sine_table, orient):
    cosine_part = jnp.einsum("ph,shrkc->sprkc", cosine, values_in, precision=HIGHEST)
    sine_part = jnp.einsum("ph,shrkc->sprkc", sine_table, values_in, precision=HIGHEST)
    real_part = cosine_part[:, :, 0] + orient * sine_part[:, :, 1]
    imag_part = cosine_part[:, :, 1] - orient * sine_part[:, :, 0]
    return jnp.stack([real_part, imag_part], axis=2)


def block_product(values_in, weights):

    def product_part(part_in, slot_index):
        return jnp.einsum("shkgi,gio->shkgo", part_in, weights[slot_index], precision=HIGHEST)

    real_input = values_in[:, :, 0]
    imag_input = values_in[:, :, 1]
    real_out = product_part(real_input, 0) - product_part(imag_input, 1)
    imag_out = product_part(imag_input, 0) + product_part(real_input, 1)
    return jnp.stack([real_out, imag_out], axis=2)


def block_adjoint(values_in, weights):

    def product_part(part_in, slot_index):
        return jnp.einsum("shkgo,gio->shkgi", part_in, weights[slot_index], precision=HIGHEST)

    real_input = values_in[:, :, 0]
    imag_input = values_in[:, :, 1]
    real_out = product_part(real_input, 0) + product_part(imag_input, 1)
    imag_out = product_part(imag_input, 0) - product_part(real_input, 1)
    return jnp.stack([real_out, imag_out], axis=2)


def weight_grad(inputs, upstream):

    def contract(left_side, right_side):
        return jnp.einsum("shkgi,shkgo->gio", left_side, right_side, precision=HIGHEST)

    real_input = inputs[:, :, 0]
    imag_input = inputs[:, :, 1]
    real_upper = upstream[:, :, 0]
    imag_upper = upstream[:, :, 1]
    first = contract(real_input, real_upper) + contract(imag_input, imag_upper)
    second = contract(real_input, imag_upper) - contract(imag_input, real_upper)
    return jnp.stack([first, second], axis=0)


def shrink(values):
    return values - SHRINK * values * lax.rsqrt(values * values + SHRINK * SHRINK)


def flat_sum(parts, axes):
    count = 1
    for name in axes:
        count *= lax.axis_size(name)
    flat = jnp.concatenate([part.reshape(-1) for part in parts])
    size = flat.shape[0]
    chunk = -(-size // (count * 8)) * 8
    flat = jnp.pad(flat, (0, count * chunk - size)).reshape(count, chunk)
    reduced = lax.all_to_all(flat, axes, 0, 0, tiled=True).sum(axis=0)
    spread = jnp.broadcast_to(reduced[None], (count, chunk))
    whole = lax.all_to_all(spread, axes, 0, 0, tiled=True).reshape(-1)
    results = []
    offset = 0
    for part in parts:
        results.append(whole[offset : offset + part.size].reshape(part.shape))
        offset += part.size
    return tuple(results)


def lat_in(values_in, cosine_in, sine_in, orient):
    cosine_part = jnp.einsum("pjh,jshmrc->sprmc", cosine_in, values_in, precision=HIGHEST)
    sine_part = jnp.einsum("pjh,jshmrc->sprmc", sine_in, values_in, precision=HIGHEST)
    real_part = cosine_part[:, :, 0] + orient * sine_part[:, :, 1]
    imag_part = cosine_part[:, :, 1] - orient * sine_part[:, :, 0]
    return jnp.stack([real_part, imag_part], axis=2)


def lat_out(values_in, cosine_out, sine_out, orient):
    cosine_part = jnp.einsum("jih,shrmc->jsimrc", cosine_out, values_in, precision=HIGHEST)
    sine_part = jnp.einsum("jih,shrmc->jsimrc", sine_out, values_in, precision=HIGHEST)
    real_part = cosine_part[:, :, :, :, 0] + orient * sine_part[:, :, :, :, 1]
    imag_part = cosine_part[:, :, :, :, 1] - orient * sine_part[:, :, :, :, 0]
    return jnp.stack([real_part, imag_part], axis=4)


def chunk_spectral(arrived, tables, weights):
    cosine_in, sine_in, cosine_out, sine_out = tables
    weight_one, bias_one, weight_two, bias_two = weights
    samples = arrived.shape[1]
    local_modes = arrived.shape[3]
    lat_rows = cosine_in.shape[0]
    groups = weight_one.shape[1]
    block_size = weight_one.shape[2]
    mode_shape = (samples, lat_rows, 2, local_modes, groups, block_size)
    row_shape = (samples, lat_rows, 2, local_modes, groups * block_size)
    spectrum = lat_in(arrived[:, :, :, :, :2], cosine_in, sine_in, 1.0).reshape(mode_shape)
    pre_inner = block_product(spectrum, weight_one) + bias_one[None, None, :, None]
    inner_act, gelu_back = jax.vjp(jax.nn.gelu, pre_inner)
    pre_outer = block_product(inner_act, weight_two) + bias_two[None, None, :, None]
    shrunk, shrink_back = jax.vjp(shrink, pre_outer)
    leaving = lat_out(shrunk.reshape(row_shape), cosine_out, sine_out, -1.0)
    shrunk_grad = lat_in(arrived[:, :, :, :, 2:], cosine_in, sine_in, 1.0).reshape(mode_shape)
    outer_grad = shrink_back(shrunk_grad)[0]
    weight_two_grad = weight_grad(inner_act, outer_grad)
    bias_two_grad = jnp.sum(outer_grad, axis=(0, 1, 3))
    inner_grad = gelu_back(block_adjoint(outer_grad, weight_two))[0]
    weight_one_grad = weight_grad(spectrum, inner_grad)
    bias_one_grad = jnp.sum(inner_grad, axis=(0, 1, 3))
    spectrum_grad = block_adjoint(inner_grad, weight_one).reshape(row_shape)
    adjoint_modes = lat_out(spectrum_grad, cosine_out, sine_out, -1.0)
    leaving_rows = jnp.concatenate([leaving, adjoint_modes], axis=4)
    return leaving_rows, (weight_one_grad, bias_one_grad, weight_two_grad, bias_two_grad)


def local(tokens, norm_gain, norm_shift, weight_one, bias_one, weight_two, bias_two, cotangent):
    lat_parts = lax.axis_size("lat")
    samples, local_rows, lon_cells, features = tokens.shape
    groups = weight_one.shape[1]
    block_size = weight_one.shape[2]
    chunks = 2 if groups % 2 == 0 else 1
    chunk_groups = groups // chunks
    chunk_width = chunk_groups * block_size
    lat_rows = local_rows * lat_parts
    kept_modes = lon_cells // 2 + 1
    padded = (kept_modes + lat_parts - 1) // lat_parts * lat_parts
    local_modes = padded // lat_parts
    lon_table = lon_basis(lon_cells, padded)
    weighted = lon_table * lon_weight(lon_cells, padded)[None, None, :]
    lon_blocks = lon_table.reshape(lon_cells, 2, lat_parts, local_modes)
    weighted_blocks = weighted.reshape(lon_cells, 2, lat_parts, local_modes)
    cosine, sine_table = lat_basis(lat_rows)
    tables = (
        cosine.reshape(lat_rows, lat_parts, local_rows),
        sine_table.reshape(lat_rows, lat_parts, local_rows),
        cosine.reshape(lat_parts, local_rows, lat_rows),
        sine_table.reshape(lat_parts, local_rows, lat_rows),
    )
    float_tokens = tokens.astype(jnp.float32)
    average = jnp.mean(float_tokens, axis=-1, keepdims=True)
    centred = float_tokens - average
    variance = jnp.mean(centred * centred, axis=-1, keepdims=True)
    inverse_std = lax.rsqrt(variance + EPSILON)
    normalized = centred * inverse_std
    normed = normalized * norm_gain + norm_shift
    upstream_out = cotangent.astype(jnp.float32)
    arrivals = []
    for index in range(chunks):
        cut = slice(index * chunk_width, (index + 1) * chunk_width)
        lon_spectrum = jnp.einsum(
            "shwc,wrjm->jshmrc", normed[..., cut], lon_blocks, precision=HIGHEST
        )
        cotangent_lon = jnp.einsum(
            "shwc,wrjm->jshmrc", upstream_out[..., cut], weighted_blocks, precision=HIGHEST
        )
        leaving_modes = jnp.concatenate([lon_spectrum, cotangent_lon], axis=4)
        arrivals.append(lax.all_to_all(leaving_modes, "lat", 0, 0, tiled=True))
    filtered_parts = []
    adjoint_parts = []
    grad_parts = []
    leaving_all = []
    for index in range(chunks):
        part = slice(index * chunk_groups, (index + 1) * chunk_groups)
        weights = (weight_one[:, part], bias_one[:, part], weight_two[:, part], bias_two[:, part])
        arrived = arrivals[index]
        if index > 0:
            arrived, leaving_all[index - 1] = lax.optimization_barrier(
                (arrived, leaving_all[index - 1])
            )
        leaving_rows, chunk_grads = chunk_spectral(arrived, tables, weights)
        leaving_all.append(leaving_rows)
        grad_parts.append(chunk_grads)
    returns = [lax.all_to_all(rows, "lat", 0, 0, tiled=True) for rows in leaving_all]
    for index in range(chunks):
        returned = returns[index]
        if index + 1 < chunks:
            returned, _ = lax.optimization_barrier((returned, leaving_all[index + 1]))
        filtered_parts.append(
            jnp.einsum(
                "jshmrc,wrjm->shwc", returned[:, :, :, :, :2], weighted_blocks, precision=HIGHEST
            )
        )
        adjoint_parts.append(
            jnp.einsum("jshmrc,wrjm->shwc", returned[:, :, :, :, 2:], lon_blocks, precision=HIGHEST)
        )
    local_grads = tuple(
        jnp.concatenate([grads[slot] for grads in grad_parts], axis=1) for slot in range(4)
    )
    filtered = jnp.concatenate(filtered_parts, axis=-1)
    block_out = (float_tokens + normed + filtered).astype(jnp.bfloat16)
    normed_grad = upstream_out + jnp.concatenate(adjoint_parts, axis=-1)
    hat_grad = normed_grad * norm_gain
    hat_mean = jnp.mean(hat_grad, axis=-1, keepdims=True)
    cross_mean = jnp.mean(hat_grad * normalized, axis=-1, keepdims=True)
    grad_input = upstream_out + inverse_std * (hat_grad - hat_mean - normalized * cross_mean)
    local_gain = jnp.sum(normed_grad * normalized, axis=(0, 1, 2))
    local_shift = jnp.sum(normed_grad, axis=(0, 1, 2))
    summed = flat_sum(local_grads + (local_gain, local_shift), ("sample", "lat"))
    spectral_grads = summed[:4]
    norm_grads = summed[4:]
    return (
        block_out,
        grad_input.astype(jnp.bfloat16),
        norm_grads[0],
        norm_grads[1],
        spectral_grads[0],
        spectral_grads[1],
        spectral_grads[2],
        spectral_grads[3],
    )


def solution(mesh):
    placed = (
        P("sample", "lat", None, None),
        P(),
        P(),
        P(),
        P(),
        P(),
        P(),
        P("sample", "lat", None, None),
    )
    return jax.shard_map(
        local,
        mesh=mesh,
        in_specs=placed,
        out_specs=(
            P("sample", "lat", None, None),
            P("sample", "lat", None, None),
            P(),
            P(),
            P(),
            P(),
            P(),
            P(),
        ),
        check_vma=False,
    )
```

```python
import jax
import jax.numpy as jnp
from jax import lax
from jax.sharding import PartitionSpec as P

HIGHEST = lax.Precision.HIGHEST
SHRINK = 0.01
EPSILON = 1e-05


def lon_basis(cell_count, mode_count):
    cell_index = jnp.arange(cell_count, dtype=jnp.int32)[:, None]
    mode_index = jnp.arange(mode_count, dtype=jnp.int32)[None, :]
    phase_int = (cell_index * mode_index % cell_count).astype(jnp.float32)
    phase_angle = phase_int * (2.0 * jnp.pi / cell_count)
    keep_scale = (mode_index < cell_count // 2 + 1).astype(jnp.float32) / jnp.sqrt(
        jnp.float32(cell_count)
    )
    return jnp.stack(
        [jnp.cos(phase_angle) * keep_scale, -jnp.sin(phase_angle) * keep_scale], axis=1
    )


def lon_weight(cell_count, mode_count):
    mode_index = jnp.arange(mode_count, dtype=jnp.int32)
    single = jnp.logical_or(mode_index == 0, 2 * mode_index == cell_count)
    return jnp.where(single, 1.0, 2.0).astype(jnp.float32)


def lat_basis(row_count):
    row_index = jnp.arange(row_count, dtype=jnp.int32)
    phase_int = (row_index[:, None] * row_index[None, :] % row_count).astype(jnp.float32)
    phase_angle = phase_int * (2.0 * jnp.pi / row_count)
    norm_factor = 1.0 / jnp.sqrt(jnp.float32(row_count))
    return (jnp.cos(phase_angle) * norm_factor, jnp.sin(phase_angle) * norm_factor)


def lat_apply(values_in, cosine, sine_table, orient):
    cosine_part = jnp.einsum("ph,shrkc->sprkc", cosine, values_in, precision=HIGHEST)
    sine_part = jnp.einsum("ph,shrkc->sprkc", sine_table, values_in, precision=HIGHEST)
    real_part = cosine_part[:, :, 0] + orient * sine_part[:, :, 1]
    imag_part = cosine_part[:, :, 1] - orient * sine_part[:, :, 0]
    return jnp.stack([real_part, imag_part], axis=2)


def block_product(values_in, weights):

    def product_part(part_in, slot_index):
        return jnp.einsum("shkgi,gio->shkgo", part_in, weights[slot_index], precision=HIGHEST)

    real_input = values_in[:, :, 0]
    imag_input = values_in[:, :, 1]
    real_out = product_part(real_input, 0) - product_part(imag_input, 1)
    imag_out = product_part(imag_input, 0) + product_part(real_input, 1)
    return jnp.stack([real_out, imag_out], axis=2)


def block_adjoint(values_in, weights):

    def product_part(part_in, slot_index):
        return jnp.einsum("shkgo,gio->shkgi", part_in, weights[slot_index], precision=HIGHEST)

    real_input = values_in[:, :, 0]
    imag_input = values_in[:, :, 1]
    real_out = product_part(real_input, 0) + product_part(imag_input, 1)
    imag_out = product_part(imag_input, 0) - product_part(real_input, 1)
    return jnp.stack([real_out, imag_out], axis=2)


def weight_grad(inputs, upstream):

    def contract(left_side, right_side):
        return jnp.einsum("shkgi,shkgo->gio", left_side, right_side, precision=HIGHEST)

    real_input = inputs[:, :, 0]
    imag_input = inputs[:, :, 1]
    real_upper = upstream[:, :, 0]
    imag_upper = upstream[:, :, 1]
    first = contract(real_input, real_upper) + contract(imag_input, imag_upper)
    second = contract(real_input, imag_upper) - contract(imag_input, real_upper)
    return jnp.stack([first, second], axis=0)


def shrink(values):
    return values - SHRINK * values * lax.rsqrt(values * values + SHRINK * SHRINK)


def flat_sum(parts, axes):
    count = 1
    for name in axes:
        count *= lax.axis_size(name)
    flat = jnp.concatenate([part.reshape(-1) for part in parts])
    size = flat.shape[0]
    chunk = -(-size // (count * 128)) * 128
    flat = jnp.pad(flat, (0, count * chunk - size)).reshape(count, chunk)
    reduced = lax.all_to_all(flat, axes, 0, 0, tiled=True).sum(axis=0)
    spread = jnp.broadcast_to(reduced[None], (count, chunk))
    whole = lax.all_to_all(spread, axes, 0, 0, tiled=True).reshape(-1)
    results = []
    offset = 0
    for part in parts:
        results.append(whole[offset : offset + part.size].reshape(part.shape))
        offset += part.size
    return tuple(results)


def lat_in(values_in, cosine_in, sine_in, orient):
    cosine_part = jnp.einsum("pjh,jshmrc->sprmc", cosine_in, values_in, precision=HIGHEST)
    sine_part = jnp.einsum("pjh,jshmrc->sprmc", sine_in, values_in, precision=HIGHEST)
    real_part = cosine_part[:, :, 0] + orient * sine_part[:, :, 1]
    imag_part = cosine_part[:, :, 1] - orient * sine_part[:, :, 0]
    return jnp.stack([real_part, imag_part], axis=2)


def lat_out(values_in, cosine_out, sine_out, orient):
    cosine_part = jnp.einsum("jih,shrmc->jsimrc", cosine_out, values_in, precision=HIGHEST)
    sine_part = jnp.einsum("jih,shrmc->jsimrc", sine_out, values_in, precision=HIGHEST)
    real_part = cosine_part[:, :, :, :, 0] + orient * sine_part[:, :, :, :, 1]
    imag_part = cosine_part[:, :, :, :, 1] - orient * sine_part[:, :, :, :, 0]
    return jnp.stack([real_part, imag_part], axis=4)


def chunk_forward(arrived, tables, weights):
    cosine_in, sine_in, cosine_out, sine_out = tables
    weight_one, bias_one, weight_two, bias_two = weights
    samples = arrived.shape[1]
    local_modes = arrived.shape[3]
    lat_rows = cosine_in.shape[0]
    groups = weight_one.shape[1]
    block_size = weight_one.shape[2]
    mode_shape = (samples, lat_rows, 2, local_modes, groups, block_size)
    row_shape = (samples, lat_rows, 2, local_modes, groups * block_size)
    spectrum = lat_in(arrived[:, :, :, :, :2], cosine_in, sine_in, 1.0).reshape(mode_shape)
    pre_inner = block_product(spectrum, weight_one) + bias_one[None, None, :, None]
    inner_act, gelu_back = jax.vjp(jax.nn.gelu, pre_inner)
    pre_outer = block_product(inner_act, weight_two) + bias_two[None, None, :, None]
    shrunk, shrink_back = jax.vjp(shrink, pre_outer)
    leaving = lat_out(shrunk.reshape(row_shape), cosine_out, sine_out, -1.0)
    return leaving, (spectrum, inner_act, gelu_back, shrink_back, mode_shape, row_shape)


def chunk_backward(arrived, saved, tables, weights):
    cosine_in, sine_in, cosine_out, sine_out = tables
    weight_one, bias_one, weight_two, bias_two = weights
    spectrum, inner_act, gelu_back, shrink_back, mode_shape, row_shape = saved
    shrunk_grad = lat_in(arrived[:, :, :, :, 2:], cosine_in, sine_in, 1.0).reshape(mode_shape)
    outer_grad = shrink_back(shrunk_grad)[0]
    weight_two_grad = weight_grad(inner_act, outer_grad)
    bias_two_grad = jnp.sum(outer_grad, axis=(0, 1, 3))
    inner_grad = gelu_back(block_adjoint(outer_grad, weight_two))[0]
    weight_one_grad = weight_grad(spectrum, inner_grad)
    bias_one_grad = jnp.sum(inner_grad, axis=(0, 1, 3))
    spectrum_grad = block_adjoint(inner_grad, weight_one).reshape(row_shape)
    adjoint_modes = lat_out(spectrum_grad, cosine_out, sine_out, -1.0)
    return adjoint_modes, (weight_one_grad, bias_one_grad, weight_two_grad, bias_two_grad)


def local(tokens, norm_gain, norm_shift, weight_one, bias_one, weight_two, bias_two, cotangent):
    lat_parts = lax.axis_size("lat")
    samples, local_rows, lon_cells, features = tokens.shape
    groups = weight_one.shape[1]
    block_size = weight_one.shape[2]
    chunks = 2 if groups % 2 == 0 else 1
    chunk_groups = groups // chunks
    chunk_width = chunk_groups * block_size
    lat_rows = local_rows * lat_parts
    kept_modes = lon_cells // 2 + 1
    padded = (kept_modes + lat_parts - 1) // lat_parts * lat_parts
    local_modes = padded // lat_parts
    lon_table = lon_basis(lon_cells, padded)
    weighted = lon_table * lon_weight(lon_cells, padded)[None, None, :]
    lon_blocks = lon_table.reshape(lon_cells, 2, lat_parts, local_modes)
    weighted_blocks = weighted.reshape(lon_cells, 2, lat_parts, local_modes)
    cosine, sine_table = lat_basis(lat_rows)
    tables = (
        cosine.reshape(lat_rows, lat_parts, local_rows),
        sine_table.reshape(lat_rows, lat_parts, local_rows),
        cosine.reshape(lat_parts, local_rows, lat_rows),
        sine_table.reshape(lat_parts, local_rows, lat_rows),
    )
    float_tokens = tokens.astype(jnp.float32)
    average = jnp.mean(float_tokens, axis=-1, keepdims=True)
    centred = float_tokens - average
    variance = jnp.mean(centred * centred, axis=-1, keepdims=True)
    inverse_std = lax.rsqrt(variance + EPSILON)
    normalized = centred * inverse_std
    normed = normalized * norm_gain + norm_shift
    upstream_out = cotangent.astype(jnp.float32)
    arrivals = []
    for index in range(chunks):
        cut = slice(index * chunk_width, (index + 1) * chunk_width)
        lon_spectrum = jnp.einsum(
            "shwc,wrjm->jshmrc", normed[..., cut], lon_blocks, precision=HIGHEST
        )
        cotangent_lon = jnp.einsum(
            "shwc,wrjm->jshmrc", upstream_out[..., cut], weighted_blocks, precision=HIGHEST
        )
        leaving_modes = jnp.concatenate([lon_spectrum, cotangent_lon], axis=4)
        arrivals.append(lax.all_to_all(leaving_modes, "lat", 0, 0, tiled=True))
    filtered_parts = []
    adjoint_parts = []
    grad_parts = []
    returns = []
    for index in range(chunks):
        part = slice(index * chunk_groups, (index + 1) * chunk_groups)
        weights = (weight_one[:, part], bias_one[:, part], weight_two[:, part], bias_two[:, part])
        arrived = arrivals[index]
        leaving, saved = chunk_forward(arrived, tables, weights)
        if index + 1 < chunks:
            arrivals[index + 1], leaving, arrived = lax.optimization_barrier(
                (arrivals[index + 1], leaving, arrived)
            )
            forward_back = lax.all_to_all(leaving, "lat", 0, 0, tiled=True)
        adjoint_modes, chunk_grads = chunk_backward(arrived, saved, tables, weights)
        grad_parts.append(chunk_grads)
        if index + 1 < chunks:
            arrivals[index + 1], adjoint_modes = lax.optimization_barrier(
                (arrivals[index + 1], adjoint_modes)
            )
            adjoint_back = lax.all_to_all(adjoint_modes, "lat", 0, 0, tiled=True)
            returns.append((forward_back, adjoint_back))
        else:
            leaving_rows = jnp.concatenate([leaving, adjoint_modes], axis=4)
            back = lax.all_to_all(leaving_rows, "lat", 0, 0, tiled=True)
            returns.append((back[:, :, :, :, :2], back[:, :, :, :, 2:]))
            last_rows = leaving_rows
    for index in range(chunks):
        forward_back, adjoint_back = returns[index]
        if index + 1 < chunks:
            forward_back, adjoint_back, _ = lax.optimization_barrier(
                (forward_back, adjoint_back, last_rows)
            )
        filtered_parts.append(
            jnp.einsum("jshmrc,wrjm->shwc", forward_back, weighted_blocks, precision=HIGHEST)
        )
        adjoint_parts.append(
            jnp.einsum("jshmrc,wrjm->shwc", adjoint_back, lon_blocks, precision=HIGHEST)
        )
    local_grads = tuple(
        jnp.concatenate([grads[slot] for grads in grad_parts], axis=1) for slot in range(4)
    )
    filtered = jnp.concatenate(filtered_parts, axis=-1)
    block_out = (float_tokens + normed + filtered).astype(jnp.bfloat16)
    normed_grad = upstream_out + jnp.concatenate(adjoint_parts, axis=-1)
    hat_grad = normed_grad * norm_gain
    hat_mean = jnp.mean(hat_grad, axis=-1, keepdims=True)
    cross_mean = jnp.mean(hat_grad * normalized, axis=-1, keepdims=True)
    grad_input = upstream_out + inverse_std * (hat_grad - hat_mean - normalized * cross_mean)
    local_gain = jnp.sum(normed_grad * normalized, axis=(0, 1, 2))
    local_shift = jnp.sum(normed_grad, axis=(0, 1, 2))
    summed = flat_sum(local_grads + (local_gain, local_shift), ("sample", "lat"))
    spectral_grads = summed[:4]
    norm_grads = summed[4:]
    return (
        block_out,
        grad_input.astype(jnp.bfloat16),
        norm_grads[0],
        norm_grads[1],
        spectral_grads[0],
        spectral_grads[1],
        spectral_grads[2],
        spectral_grads[3],
    )


def solution(mesh):
    placed = (
        P("sample", "lat", None, None),
        P(),
        P(),
        P(),
        P(),
        P(),
        P(),
        P("sample", "lat", None, None),
    )
    return jax.shard_map(
        local,
        mesh=mesh,
        in_specs=placed,
        out_specs=(
            P("sample", "lat", None, None),
            P("sample", "lat", None, None),
            P(),
            P(),
            P(),
            P(),
            P(),
            P(),
        ),
        check_vma=False,
    )
```

```python
import jax
import jax.numpy as jnp
from jax import lax
from jax.sharding import PartitionSpec as P

HIGHEST = lax.Precision.HIGHEST
SHRINK = 0.01
EPSILON = 1e-05


def lon_basis(cell_count, mode_count):
    cell_index = jnp.arange(cell_count, dtype=jnp.int32)[:, None]
    mode_index = jnp.arange(mode_count, dtype=jnp.int32)[None, :]
    phase_int = (cell_index * mode_index % cell_count).astype(jnp.float32)
    phase_angle = phase_int * (2.0 * jnp.pi / cell_count)
    keep_scale = (mode_index < cell_count // 2 + 1).astype(jnp.float32) / jnp.sqrt(
        jnp.float32(cell_count)
    )
    return jnp.stack(
        [jnp.cos(phase_angle) * keep_scale, -jnp.sin(phase_angle) * keep_scale], axis=1
    )


def lon_weight(cell_count, mode_count):
    mode_index = jnp.arange(mode_count, dtype=jnp.int32)
    single = jnp.logical_or(mode_index == 0, 2 * mode_index == cell_count)
    return jnp.where(single, 1.0, 2.0).astype(jnp.float32)


def lat_basis(row_count):
    row_index = jnp.arange(row_count, dtype=jnp.int32)
    phase_int = (row_index[:, None] * row_index[None, :] % row_count).astype(jnp.float32)
    phase_angle = phase_int * (2.0 * jnp.pi / row_count)
    norm_factor = 1.0 / jnp.sqrt(jnp.float32(row_count))
    return (jnp.cos(phase_angle) * norm_factor, jnp.sin(phase_angle) * norm_factor)


def lat_apply(values_in, cosine, sine_table, orient):
    cosine_part = jnp.einsum("ph,shrkc->sprkc", cosine, values_in, precision=HIGHEST)
    sine_part = jnp.einsum("ph,shrkc->sprkc", sine_table, values_in, precision=HIGHEST)
    real_part = cosine_part[:, :, 0] + orient * sine_part[:, :, 1]
    imag_part = cosine_part[:, :, 1] - orient * sine_part[:, :, 0]
    return jnp.stack([real_part, imag_part], axis=2)


def block_product(values_in, weights):
    real_weight, imag_weight = weights[0], weights[1]
    paired = jnp.stack(
        [
            jnp.stack([real_weight, imag_weight], axis=2),
            jnp.stack([-imag_weight, real_weight], axis=2),
        ],
        axis=1,
    )
    return jnp.einsum("shrkgi,griuo->shukgo", values_in, paired, precision=HIGHEST)


def block_adjoint(values_in, weights):
    real_weight, imag_weight = weights[0], weights[1]
    paired = jnp.stack(
        [
            jnp.stack([real_weight, -imag_weight], axis=1),
            jnp.stack([imag_weight, real_weight], axis=1),
        ],
        axis=1,
    )
    return jnp.einsum("shrkgo,gruio->shukgi", values_in, paired, precision=HIGHEST)


def weight_grad(inputs, upstream):

    def contract(left_side, right_side):
        return jnp.einsum("shkgi,shkgo->gio", left_side, right_side, precision=HIGHEST)

    real_input = inputs[:, :, 0]
    imag_input = inputs[:, :, 1]
    real_upper = upstream[:, :, 0]
    imag_upper = upstream[:, :, 1]
    first = contract(real_input, real_upper) + contract(imag_input, imag_upper)
    second = contract(real_input, imag_upper) - contract(imag_input, real_upper)
    return jnp.stack([first, second], axis=0)


def shrink(values):
    return values - SHRINK * values * lax.rsqrt(values * values + SHRINK * SHRINK)


def flat_sum(parts, axes):
    count = 1
    for name in axes:
        count *= lax.axis_size(name)
    flat = jnp.concatenate([part.reshape(-1) for part in parts])
    size = flat.shape[0]
    chunk = -(-size // (count * 128)) * 128
    flat = jnp.pad(flat, (0, count * chunk - size)).reshape(count, chunk)
    reduced = lax.all_to_all(flat, axes, 0, 0, tiled=True).sum(axis=0)
    spread = jnp.broadcast_to(reduced[None], (count, chunk))
    whole = lax.all_to_all(spread, axes, 0, 0, tiled=True).reshape(-1)
    results = []
    offset = 0
    for part in parts:
        results.append(whole[offset : offset + part.size].reshape(part.shape))
        offset += part.size
    return tuple(results)


def lat_in(values_in, cosine_in, sine_in, orient):
    cosine_part = jnp.einsum("pjh,jshmrc->sprmc", cosine_in, values_in, precision=HIGHEST)
    sine_part = jnp.einsum("pjh,jshmrc->sprmc", sine_in, values_in, precision=HIGHEST)
    real_part = cosine_part[:, :, 0] + orient * sine_part[:, :, 1]
    imag_part = cosine_part[:, :, 1] - orient * sine_part[:, :, 0]
    return jnp.stack([real_part, imag_part], axis=2)


def lat_out(values_in, cosine_out, sine_out, orient):
    cosine_part = jnp.einsum("jih,shrmc->jsimrc", cosine_out, values_in, precision=HIGHEST)
    sine_part = jnp.einsum("jih,shrmc->jsimrc", sine_out, values_in, precision=HIGHEST)
    real_part = cosine_part[:, :, :, :, 0] + orient * sine_part[:, :, :, :, 1]
    imag_part = cosine_part[:, :, :, :, 1] - orient * sine_part[:, :, :, :, 0]
    return jnp.stack([real_part, imag_part], axis=4)


def chunk_spectral(arrived, tables, weights):
    cosine_in, sine_in, cosine_out, sine_out = tables
    weight_one, bias_one, weight_two, bias_two = weights
    samples = arrived.shape[1]
    local_modes = arrived.shape[3]
    lat_rows = cosine_in.shape[0]
    groups = weight_one.shape[1]
    block_size = weight_one.shape[2]
    mode_shape = (samples, lat_rows, 2, local_modes, groups, block_size)
    row_shape = (samples, lat_rows, 2, local_modes, groups * block_size)
    spectrum = lat_in(arrived[:, :, :, :, :2], cosine_in, sine_in, 1.0).reshape(mode_shape)
    pre_inner = block_product(spectrum, weight_one) + bias_one[None, None, :, None]
    inner_act, gelu_back = jax.vjp(jax.nn.gelu, pre_inner)
    pre_outer = block_product(inner_act, weight_two) + bias_two[None, None, :, None]
    shrunk, shrink_back = jax.vjp(shrink, pre_outer)
    leaving = lat_out(shrunk.reshape(row_shape), cosine_out, sine_out, -1.0)
    shrunk_grad = lat_in(arrived[:, :, :, :, 2:], cosine_in, sine_in, 1.0).reshape(mode_shape)
    outer_grad = shrink_back(shrunk_grad)[0]
    weight_two_grad = weight_grad(inner_act, outer_grad)
    bias_two_grad = jnp.sum(outer_grad, axis=(0, 1, 3))
    inner_grad = gelu_back(block_adjoint(outer_grad, weight_two))[0]
    weight_one_grad = weight_grad(spectrum, inner_grad)
    bias_one_grad = jnp.sum(inner_grad, axis=(0, 1, 3))
    spectrum_grad = block_adjoint(inner_grad, weight_one).reshape(row_shape)
    adjoint_modes = lat_out(spectrum_grad, cosine_out, sine_out, -1.0)
    leaving_rows = jnp.concatenate([leaving, adjoint_modes], axis=4)
    return leaving_rows, (weight_one_grad, bias_one_grad, weight_two_grad, bias_two_grad)


def local(tokens, norm_gain, norm_shift, weight_one, bias_one, weight_two, bias_two, cotangent):
    lat_parts = lax.axis_size("lat")
    samples, local_rows, lon_cells, features = tokens.shape
    groups = weight_one.shape[1]
    block_size = weight_one.shape[2]
    chunks = 2 if groups % 2 == 0 else 1
    chunk_groups = groups // chunks
    chunk_width = chunk_groups * block_size
    lat_rows = local_rows * lat_parts
    kept_modes = lon_cells // 2 + 1
    padded = (kept_modes + lat_parts - 1) // lat_parts * lat_parts
    local_modes = padded // lat_parts
    lon_table = lon_basis(lon_cells, padded)
    weighted = lon_table * lon_weight(lon_cells, padded)[None, None, :]
    lon_blocks = lon_table.reshape(lon_cells, 2, lat_parts, local_modes)
    weighted_blocks = weighted.reshape(lon_cells, 2, lat_parts, local_modes)
    cosine, sine_table = lat_basis(lat_rows)
    tables = (
        cosine.reshape(lat_rows, lat_parts, local_rows),
        sine_table.reshape(lat_rows, lat_parts, local_rows),
        cosine.reshape(lat_parts, local_rows, lat_rows),
        sine_table.reshape(lat_parts, local_rows, lat_rows),
    )
    float_tokens = tokens.astype(jnp.float32)
    average = jnp.mean(float_tokens, axis=-1, keepdims=True)
    centred = float_tokens - average
    variance = jnp.mean(centred * centred, axis=-1, keepdims=True)
    inverse_std = lax.rsqrt(variance + EPSILON)
    normalized = centred * inverse_std
    normed = normalized * norm_gain + norm_shift
    upstream_out = cotangent.astype(jnp.float32)
    arrivals = []
    for index in range(chunks):
        cut = slice(index * chunk_width, (index + 1) * chunk_width)
        lon_spectrum = jnp.einsum(
            "shwc,wrjm->jshmrc", normed[..., cut], lon_blocks, precision=HIGHEST
        )
        cotangent_lon = jnp.einsum(
            "shwc,wrjm->jshmrc", upstream_out[..., cut], weighted_blocks, precision=HIGHEST
        )
        leaving_modes = jnp.concatenate([lon_spectrum, cotangent_lon], axis=4)
        arrivals.append(lax.all_to_all(leaving_modes, "lat", 0, 0, tiled=True))
    filtered_parts = []
    adjoint_parts = []
    grad_parts = []
    leaving_all = []
    for index in range(chunks):
        part = slice(index * chunk_groups, (index + 1) * chunk_groups)
        weights = (weight_one[:, part], bias_one[:, part], weight_two[:, part], bias_two[:, part])
        arrived = arrivals[index]
        if index > 0:
            arrived, leaving_all[index - 1] = lax.optimization_barrier(
                (arrived, leaving_all[index - 1])
            )
        leaving_rows, chunk_grads = chunk_spectral(arrived, tables, weights)
        leaving_all.append(leaving_rows)
        grad_parts.append(chunk_grads)
    returns = [lax.all_to_all(rows, "lat", 0, 0, tiled=True) for rows in leaving_all]
    for index in range(chunks):
        returned = returns[index]
        if index + 1 < chunks:
            returned, _ = lax.optimization_barrier((returned, leaving_all[index + 1]))
        filtered_parts.append(
            jnp.einsum(
                "jshmrc,wrjm->shwc", returned[:, :, :, :, :2], weighted_blocks, precision=HIGHEST
            )
        )
        adjoint_parts.append(
            jnp.einsum("jshmrc,wrjm->shwc", returned[:, :, :, :, 2:], lon_blocks, precision=HIGHEST)
        )
    local_grads = tuple(
        jnp.concatenate([grads[slot] for grads in grad_parts], axis=1) for slot in range(4)
    )
    filtered = jnp.concatenate(filtered_parts, axis=-1)
    block_out = (float_tokens + normed + filtered).astype(jnp.bfloat16)
    normed_grad = upstream_out + jnp.concatenate(adjoint_parts, axis=-1)
    hat_grad = normed_grad * norm_gain
    hat_mean = jnp.mean(hat_grad, axis=-1, keepdims=True)
    cross_mean = jnp.mean(hat_grad * normalized, axis=-1, keepdims=True)
    grad_input = upstream_out + inverse_std * (hat_grad - hat_mean - normalized * cross_mean)
    local_gain = jnp.sum(normed_grad * normalized, axis=(0, 1, 2))
    local_shift = jnp.sum(normed_grad, axis=(0, 1, 2))
    summed = flat_sum(local_grads + (local_gain, local_shift), ("sample", "lat"))
    spectral_grads = summed[:4]
    norm_grads = summed[4:]
    return (
        block_out,
        grad_input.astype(jnp.bfloat16),
        norm_grads[0],
        norm_grads[1],
        spectral_grads[0],
        spectral_grads[1],
        spectral_grads[2],
        spectral_grads[3],
    )


def solution(mesh):
    placed = (
        P("sample", "lat", None, None),
        P(),
        P(),
        P(),
        P(),
        P(),
        P(),
        P("sample", "lat", None, None),
    )
    return jax.shard_map(
        local,
        mesh=mesh,
        in_specs=placed,
        out_specs=(
            P("sample", "lat", None, None),
            P("sample", "lat", None, None),
            P(),
            P(),
            P(),
            P(),
            P(),
            P(),
        ),
        check_vma=False,
    )
```

```python
import jax
import jax.numpy as jnp
from jax import lax
from jax.sharding import PartitionSpec as P

HIGHEST = lax.Precision.HIGHEST
SHRINK = 0.01
EPSILON = 1e-05


def lon_basis(cell_count, mode_count):
    cell_index = jnp.arange(cell_count, dtype=jnp.int32)[:, None]
    mode_index = jnp.arange(mode_count, dtype=jnp.int32)[None, :]
    phase_int = (cell_index * mode_index % cell_count).astype(jnp.float32)
    phase_angle = phase_int * (2.0 * jnp.pi / cell_count)
    keep_scale = (mode_index < cell_count // 2 + 1).astype(jnp.float32) / jnp.sqrt(
        jnp.float32(cell_count)
    )
    return jnp.stack(
        [jnp.cos(phase_angle) * keep_scale, -jnp.sin(phase_angle) * keep_scale], axis=1
    )


def lon_weight(cell_count, mode_count):
    mode_index = jnp.arange(mode_count, dtype=jnp.int32)
    single = jnp.logical_or(mode_index == 0, 2 * mode_index == cell_count)
    return jnp.where(single, 1.0, 2.0).astype(jnp.float32)


def lat_basis(row_count):
    row_index = jnp.arange(row_count, dtype=jnp.int32)
    phase_int = (row_index[:, None] * row_index[None, :] % row_count).astype(jnp.float32)
    phase_angle = phase_int * (2.0 * jnp.pi / row_count)
    norm_factor = 1.0 / jnp.sqrt(jnp.float32(row_count))
    return (jnp.cos(phase_angle) * norm_factor, jnp.sin(phase_angle) * norm_factor)


def lat_apply(values_in, cosine, sine_table, orient):
    cosine_part = jnp.einsum("ph,shrkc->sprkc", cosine, values_in, precision=HIGHEST)
    sine_part = jnp.einsum("ph,shrkc->sprkc", sine_table, values_in, precision=HIGHEST)
    real_part = cosine_part[:, :, 0] + orient * sine_part[:, :, 1]
    imag_part = cosine_part[:, :, 1] - orient * sine_part[:, :, 0]
    return jnp.stack([real_part, imag_part], axis=2)


def block_product(values_in, weights):
    real_weight, imag_weight = weights[0], weights[1]
    paired = jnp.stack(
        [
            jnp.stack([real_weight, imag_weight], axis=2),
            jnp.stack([-imag_weight, real_weight], axis=2),
        ],
        axis=1,
    )
    return jnp.einsum("shrkgi,griuo->shukgo", values_in, paired, precision=HIGHEST)


def block_adjoint(values_in, weights):
    real_weight, imag_weight = weights[0], weights[1]
    paired = jnp.stack(
        [
            jnp.stack([real_weight, -imag_weight], axis=1),
            jnp.stack([imag_weight, real_weight], axis=1),
        ],
        axis=1,
    )
    return jnp.einsum("shrkgo,gruio->shukgi", values_in, paired, precision=HIGHEST)


def weight_grad(inputs, upstream):
    full = jnp.einsum("shrkgi,shukgo->rugio", inputs, upstream, precision=HIGHEST)
    first = full[0, 0] + full[1, 1]
    second = full[0, 1] - full[1, 0]
    return jnp.stack([first, second], axis=0)


def shrink(values):
    return values - SHRINK * values * lax.rsqrt(values * values + SHRINK * SHRINK)


def flat_sum(parts, axes):
    count = 1
    for name in axes:
        count *= lax.axis_size(name)
    flat = jnp.concatenate([part.reshape(-1) for part in parts])
    size = flat.shape[0]
    chunk = -(-size // (count * 128)) * 128
    flat = jnp.pad(flat, (0, count * chunk - size)).reshape(count, chunk)
    reduced = lax.all_to_all(flat, axes, 0, 0, tiled=True).sum(axis=0)
    spread = jnp.broadcast_to(reduced[None], (count, chunk))
    whole = lax.all_to_all(spread, axes, 0, 0, tiled=True).reshape(-1)
    results = []
    offset = 0
    for part in parts:
        results.append(whole[offset : offset + part.size].reshape(part.shape))
        offset += part.size
    return tuple(results)


def lat_in(values_in, cosine_in, sine_in, orient):
    cosine_part = jnp.einsum("pjh,jshmrc->sprmc", cosine_in, values_in, precision=HIGHEST)
    sine_part = jnp.einsum("pjh,jshmrc->sprmc", sine_in, values_in, precision=HIGHEST)
    real_part = cosine_part[:, :, 0] + orient * sine_part[:, :, 1]
    imag_part = cosine_part[:, :, 1] - orient * sine_part[:, :, 0]
    return jnp.stack([real_part, imag_part], axis=2)


def lat_out(values_in, cosine_out, sine_out, orient):
    cosine_part = jnp.einsum("jih,shrmc->jsimrc", cosine_out, values_in, precision=HIGHEST)
    sine_part = jnp.einsum("jih,shrmc->jsimrc", sine_out, values_in, precision=HIGHEST)
    real_part = cosine_part[:, :, :, :, 0] + orient * sine_part[:, :, :, :, 1]
    imag_part = cosine_part[:, :, :, :, 1] - orient * sine_part[:, :, :, :, 0]
    return jnp.stack([real_part, imag_part], axis=4)


def chunk_spectral(arrived, tables, weights):
    cosine_in, sine_in, cosine_out, sine_out = tables
    weight_one, bias_one, weight_two, bias_two = weights
    samples = arrived.shape[1]
    local_modes = arrived.shape[3]
    lat_rows = cosine_in.shape[0]
    groups = weight_one.shape[1]
    block_size = weight_one.shape[2]
    mode_shape = (samples, lat_rows, 2, local_modes, groups, block_size)
    row_shape = (samples, lat_rows, 2, local_modes, groups * block_size)
    spectrum = lat_in(arrived[:, :, :, :, :2], cosine_in, sine_in, 1.0).reshape(mode_shape)
    pre_inner = block_product(spectrum, weight_one) + bias_one[None, None, :, None]
    inner_act, gelu_back = jax.vjp(jax.nn.gelu, pre_inner)
    pre_outer = block_product(inner_act, weight_two) + bias_two[None, None, :, None]
    shrunk, shrink_back = jax.vjp(shrink, pre_outer)
    leaving = lat_out(shrunk.reshape(row_shape), cosine_out, sine_out, -1.0)
    shrunk_grad = lat_in(arrived[:, :, :, :, 2:], cosine_in, sine_in, 1.0).reshape(mode_shape)
    outer_grad = shrink_back(shrunk_grad)[0]
    weight_two_grad = weight_grad(inner_act, outer_grad)
    bias_two_grad = jnp.sum(outer_grad, axis=(0, 1, 3))
    inner_grad = gelu_back(block_adjoint(outer_grad, weight_two))[0]
    weight_one_grad = weight_grad(spectrum, inner_grad)
    bias_one_grad = jnp.sum(inner_grad, axis=(0, 1, 3))
    spectrum_grad = block_adjoint(inner_grad, weight_one).reshape(row_shape)
    adjoint_modes = lat_out(spectrum_grad, cosine_out, sine_out, -1.0)
    leaving_rows = jnp.concatenate([leaving, adjoint_modes], axis=4)
    return leaving_rows, (weight_one_grad, bias_one_grad, weight_two_grad, bias_two_grad)


def local(tokens, norm_gain, norm_shift, weight_one, bias_one, weight_two, bias_two, cotangent):
    lat_parts = lax.axis_size("lat")
    samples, local_rows, lon_cells, features = tokens.shape
    groups = weight_one.shape[1]
    block_size = weight_one.shape[2]
    chunks = 2 if groups % 2 == 0 else 1
    chunk_groups = groups // chunks
    chunk_width = chunk_groups * block_size
    lat_rows = local_rows * lat_parts
    kept_modes = lon_cells // 2 + 1
    padded = (kept_modes + lat_parts - 1) // lat_parts * lat_parts
    local_modes = padded // lat_parts
    lon_table = lon_basis(lon_cells, padded)
    weighted = lon_table * lon_weight(lon_cells, padded)[None, None, :]
    lon_blocks = lon_table.reshape(lon_cells, 2, lat_parts, local_modes)
    weighted_blocks = weighted.reshape(lon_cells, 2, lat_parts, local_modes)
    cosine, sine_table = lat_basis(lat_rows)
    tables = (
        cosine.reshape(lat_rows, lat_parts, local_rows),
        sine_table.reshape(lat_rows, lat_parts, local_rows),
        cosine.reshape(lat_parts, local_rows, lat_rows),
        sine_table.reshape(lat_parts, local_rows, lat_rows),
    )
    float_tokens = tokens.astype(jnp.float32)
    average = jnp.mean(float_tokens, axis=-1, keepdims=True)
    centred = float_tokens - average
    variance = jnp.mean(centred * centred, axis=-1, keepdims=True)
    inverse_std = lax.rsqrt(variance + EPSILON)
    normalized = centred * inverse_std
    normed = normalized * norm_gain + norm_shift
    upstream_out = cotangent.astype(jnp.float32)
    arrivals = []
    for index in range(chunks):
        cut = slice(index * chunk_width, (index + 1) * chunk_width)
        lon_spectrum = jnp.einsum(
            "shwc,wrjm->jshmrc", normed[..., cut], lon_blocks, precision=HIGHEST
        )
        cotangent_lon = jnp.einsum(
            "shwc,wrjm->jshmrc", upstream_out[..., cut], weighted_blocks, precision=HIGHEST
        )
        leaving_modes = jnp.concatenate([lon_spectrum, cotangent_lon], axis=4)
        arrivals.append(lax.all_to_all(leaving_modes, "lat", 0, 0, tiled=True))
    filtered_parts = []
    adjoint_parts = []
    grad_parts = []
    leaving_all = []
    for index in range(chunks):
        part = slice(index * chunk_groups, (index + 1) * chunk_groups)
        weights = (weight_one[:, part], bias_one[:, part], weight_two[:, part], bias_two[:, part])
        arrived = arrivals[index]
        if index > 0:
            arrived, leaving_all[index - 1] = lax.optimization_barrier(
                (arrived, leaving_all[index - 1])
            )
        leaving_rows, chunk_grads = chunk_spectral(arrived, tables, weights)
        leaving_all.append(leaving_rows)
        grad_parts.append(chunk_grads)
    returns = [lax.all_to_all(rows, "lat", 0, 0, tiled=True) for rows in leaving_all]
    for index in range(chunks):
        returned = returns[index]
        if index + 1 < chunks:
            returned, _ = lax.optimization_barrier((returned, leaving_all[index + 1]))
        filtered_parts.append(
            jnp.einsum(
                "jshmrc,wrjm->shwc", returned[:, :, :, :, :2], weighted_blocks, precision=HIGHEST
            )
        )
        adjoint_parts.append(
            jnp.einsum("jshmrc,wrjm->shwc", returned[:, :, :, :, 2:], lon_blocks, precision=HIGHEST)
        )
    local_grads = tuple(
        jnp.concatenate([grads[slot] for grads in grad_parts], axis=1) for slot in range(4)
    )
    filtered = jnp.concatenate(filtered_parts, axis=-1)
    block_out = (float_tokens + normed + filtered).astype(jnp.bfloat16)
    normed_grad = upstream_out + jnp.concatenate(adjoint_parts, axis=-1)
    hat_grad = normed_grad * norm_gain
    hat_mean = jnp.mean(hat_grad, axis=-1, keepdims=True)
    cross_mean = jnp.mean(hat_grad * normalized, axis=-1, keepdims=True)
    grad_input = upstream_out + inverse_std * (hat_grad - hat_mean - normalized * cross_mean)
    local_gain = jnp.sum(normed_grad * normalized, axis=(0, 1, 2))
    local_shift = jnp.sum(normed_grad, axis=(0, 1, 2))
    summed = flat_sum(local_grads + (local_gain, local_shift), ("sample", "lat"))
    spectral_grads = summed[:4]
    norm_grads = summed[4:]
    return (
        block_out,
        grad_input.astype(jnp.bfloat16),
        norm_grads[0],
        norm_grads[1],
        spectral_grads[0],
        spectral_grads[1],
        spectral_grads[2],
        spectral_grads[3],
    )


def solution(mesh):
    placed = (
        P("sample", "lat", None, None),
        P(),
        P(),
        P(),
        P(),
        P(),
        P(),
        P("sample", "lat", None, None),
    )
    return jax.shard_map(
        local,
        mesh=mesh,
        in_specs=placed,
        out_specs=(
            P("sample", "lat", None, None),
            P("sample", "lat", None, None),
            P(),
            P(),
            P(),
            P(),
            P(),
            P(),
        ),
        check_vma=False,
    )
```
